32 devices in a mesh: ctx: 8 (over y, x, core), tp: 4 (over z).
Axes of the slice: x: 2, y: 2, z: 4, core: 2. Of those that a mesh axis runs over, the one named last changes fastest.
Arguments:
- qkv_input: bfloat16 [8192, 8192], P('ctx', 'tp'), may hold values from -48 to 48
- conv_weight: bfloat16 [4, 8192], P(None, 'tp'), may hold values from -3 to 3
- log_decay: float32 [32, 8192], P('tp', 'ctx'), may hold values from -1 to 0
- beta_gate: float32 [32, 8192], P('tp', 'ctx'), may hold values from 0.05 to 0.95
- output_gate: bfloat16 [8192, 4096], P('ctx', 'tp'), may hold values from -6 to 6
- norm_gain: float32 [128], replicated, may hold values from 0.25 to 1.75
- out_weight: bfloat16 [4096, 2048], P('tp'), may hold values from -0.09375 to 0.09375
Outputs:
- layer_out: bfloat16 [8192, 2048], P(('ctx', 'tp'))
The draws below stay inside these ranges and needn't reach their ends.
All inputs are finite; a program needn't handle non-finite values.
Results may differ from the reference program's by a relative error of at most 0.015.
Values may be sent and summed in bfloat16 or wider, within the bound.
No kernel may reach another device: no remote copies, remote signals or barrier semaphores. Data moves between devices by JAX's collectives and lax.ppermute only.
A program may use at most 128 MiB of HBM per device.

```python
import jax
import jax.numpy as jnp
from jax import lax

DMODEL = 2048
VALUE_HEADS = 32
HK = 16
DK = 128
DV = 128
KCONV = 4
BLOCK = 64
TOK_DEV = 1024
CHAN = 8192
VCH = 4096
TOKEN_POSITIONS = 8192
N_TP = 4


def draw_qkv_input(key, part):
    head_ratio = VALUE_HEADS // HK
    group_width = 2 * DK + head_ratio * DV
    parallel_lanes = jax.random.split(key, 3)
    channel_pos = jnp.arange(CHAN) % group_width
    qk_scale = jnp.exp(jax.random.uniform(parallel_lanes[0], (CHAN,), jnp.float32, jnp.log(0.01), 0.0))
    value_scale = jnp.exp(jax.random.uniform(parallel_lanes[1], (CHAN,), jnp.float32, jnp.log(0.3), jnp.log(3.0)))
    channel_scale = jnp.where(channel_pos >= 2 * DK, value_scale, qk_scale)
    entries = jnp.clip(jax.random.normal(parallel_lanes[2], (TOKEN_POSITIONS, CHAN), jnp.float32), -6.0, 6.0)
    return (entries * channel_scale).astype(jnp.bfloat16)


def draw_log_decay(key, part):
    parallel_lanes = jax.random.split(key, 7)
    fast_share = 0.5
    fast_heads = jax.random.uniform(parallel_lanes[0], (VALUE_HEADS, 1), jnp.float32) < fast_share
    fast_rate = jnp.exp(jax.random.uniform(parallel_lanes[1], (VALUE_HEADS, 1), jnp.float32, jnp.log(1.0 / 50.0), jnp.log(1.0 / 30.0)))
    slow_rate = 2.3 / TOKEN_POSITIONS * jax.random.uniform(parallel_lanes[2], (VALUE_HEADS, 1), jnp.float32, 0.1, 0.5)
    base_rate = jnp.where(fast_heads, fast_rate, slow_rate)[:, :, None]
    device_factor = jnp.exp(jax.random.uniform(parallel_lanes[3], (VALUE_HEADS, TOKEN_POSITIONS // TOK_DEV, 1), jnp.float32, jnp.log(0.5), jnp.log(2.0)))
    rough_factor = jnp.exp(jax.random.uniform(parallel_lanes[4], (VALUE_HEADS, TOKEN_POSITIONS // TOK_DEV, TOK_DEV), jnp.float32, jnp.log(0.5), jnp.log(2.0)))
    decay_speeds = (base_rate * device_factor * rough_factor).reshape(VALUE_HEADS, TOKEN_POSITIONS)
    window_matched = jax.random.uniform(parallel_lanes[5], (VALUE_HEADS, TOKEN_POSITIONS), jnp.float32) < 3.0 / TOKEN_POSITIONS
    window_length = jax.random.uniform(parallel_lanes[6], (VALUE_HEADS, TOKEN_POSITIONS), jnp.float32, jnp.log(1.25), jnp.log(2.0))
    return -(decay_speeds + jnp.where(window_matched, window_length, 0.0))


def block_levels(stream_key, extent, cuts, least, largest):
    def one(dim, blocks):
        steps = jax.random.uniform(jax.random.fold_in(jax.random.fold_in(stream_key, 6), dim), (blocks,), jnp.float32, least / len(cuts), largest / len(cuts))
        return jnp.repeat(jnp.exp(steps), extent[dim] // blocks).reshape((-1,) + (1,) * (len(extent) - dim - 1))

    factor_of = one(*cuts[0])
    for cut in cuts[1:]:
        factor_of = factor_of * one(*cut)
    return factor_of


def gaussian(own_key, dims, width, bound, pieces=(), kind=jnp.bfloat16):
    factor_of = block_levels(own_key, dims, pieces, -0.22, 0.18) if pieces else 1.0
    values = jax.random.normal(own_key, dims, jnp.float32) * width * factor_of
    return jnp.minimum(jnp.maximum(values, -bound), bound).astype(kind)


def setup_inputs(seed: int = 0) -> dict:
    key_of = jax.random.split(jax.random.key(seed), 8)
    qkv_input = draw_qkv_input(jax.random.fold_in(key_of[7], 71), 0)
    conv_weight = gaussian(key_of[1], (KCONV, CHAN), KCONV ** -0.5, 3.0, ((1, 4),))
    log_decay = draw_log_decay(jax.random.fold_in(key_of[7], 71), 0)
    beta_gate = jnp.clip(0.05 + 0.9 * jax.random.uniform(key_of[3], (VALUE_HEADS, TOKEN_POSITIONS), jnp.float32) ** block_levels(key_of[3], (VALUE_HEADS, TOKEN_POSITIONS), ((0, 4), (1, 8)), -0.2, 0.2), 0.05, 0.95)
    output_gate = gaussian(key_of[4], (TOKEN_POSITIONS, VCH), 1.0, 6.0, ((0, 8), (1, 4)))
    norm_gain = jnp.clip(1.0 + 0.15 * jax.random.normal(key_of[5], (DV,), jnp.float32), 0.25, 1.75)
    out_weight = gaussian(key_of[6], (VCH, DMODEL), VCH ** -0.5, 0.09375, ((0, 4),))
    return {"qkv_input": qkv_input, "conv_weight": conv_weight, "log_decay": log_decay, "beta_gate": beta_gate, "output_gate": output_gate, "norm_gain": norm_gain, "out_weight": out_weight}


exact_matmul_mode = lax.Precision.HIGHEST

def l2_rows(tensor):
    return tensor * lax.rsqrt(lax.optimization_barrier(jnp.sum(tensor * tensor, axis=-1, keepdims=True)) + 1e-06)

def run_head(queries, key_rows, values, decays, strengths):
    position = jnp.arange(BLOCK)
    lower_mask = position[:, None] >= position[None, :]
    strict_mask = position[:, None] > position[None, :]
    identity_block = jnp.eye(BLOCK, dtype=jnp.float32)

    def step_block(present_state, block_item):
        query_low, key_low, value_low, block_decay, block_beta = block_item
        block_query = query_low.astype(jnp.float32)
        block_key = key_low.astype(jnp.float32)
        block_value = value_low.astype(jnp.float32)
        cumulative = jnp.cumsum(block_decay)
        exponent = jnp.where(lower_mask, cumulative[:, None] - cumulative[None, :], 0.0)
        damping = jnp.where(lower_mask, jnp.exp(exponent), 0.0)
        key_gram = jnp.dot(key_low.astype(jnp.float32), key_low.T.astype(jnp.float32), preferred_element_type=jnp.float32)
        system = identity_block + jnp.where(strict_mask, block_beta[:, None] * key_gram * damping, 0.0)
        fresh_values = jax.scipy.linalg.solve_triangular(system, block_beta[:, None] * block_value, lower=True, unit_diagonal=True)
        wy_weights = jax.scipy.linalg.solve_triangular(system, (block_beta * jnp.exp(cumulative))[:, None] * block_key, lower=True, unit_diagonal=True)
        updated_value_rows = fresh_values - jnp.dot(wy_weights, present_state, precision=exact_matmul_mode)
        scores = jnp.dot(query_low.astype(jnp.float32), key_low.T.astype(jnp.float32), preferred_element_type=jnp.float32) * damping
        emitted_output = jnp.dot(jnp.exp(cumulative)[:, None] * block_query, present_state, precision=exact_matmul_mode)
        emitted_output = emitted_output + jnp.dot(scores, updated_value_rows, precision=exact_matmul_mode)
        key_decayed = jnp.exp(cumulative[-1] - cumulative)[:, None] * block_key
        present_state = jnp.exp(cumulative[-1]) * present_state + jnp.dot(key_decayed.T, updated_value_rows, precision=exact_matmul_mode)
        return (present_state, emitted_output)
    initial = jnp.zeros((DK, DV), jnp.float32)
    _, outputs = lax.scan(step_block, initial, (queries, key_rows, values, decays, strengths))
    return outputs.reshape(-1, DV)

def reference(qkv_input, conv_weight, log_decay, beta_gate, output_gate, norm_gain, out_weight):
    head_ratio = VALUE_HEADS // HK
    group_width = 2 * DK + head_ratio * DV
    block_count = TOKEN_POSITIONS // BLOCK

    def group_out(group_index):
        col_start = group_index * group_width
        raw_cols = lax.dynamic_slice_in_dim(qkv_input, col_start, group_width, 1).astype(jnp.float32)
        conv_cols = lax.dynamic_slice_in_dim(conv_weight, col_start, group_width, 1).astype(jnp.float32)
        padded = jnp.concatenate([jnp.zeros((KCONV - 1, group_width), jnp.float32), raw_cols], 0)
        mixed = conv_cols[0] * padded[0:TOKEN_POSITIONS]
        for offset in range(1, KCONV):
            mixed = mixed + conv_cols[offset] * padded[offset:offset + TOKEN_POSITIONS]
        mixed = jax.nn.silu(mixed)
        queries = (l2_rows(mixed[:, :DK]) * DK ** (-0.5)).astype(jnp.bfloat16)
        key_rows = l2_rows(mixed[:, DK:2 * DK]).astype(jnp.bfloat16)
        values = mixed[:, 2 * DK:].astype(jnp.bfloat16).reshape(TOKEN_POSITIONS, head_ratio, DV).transpose(1, 0, 2)
        decays = lax.dynamic_slice_in_dim(log_decay, group_index * head_ratio, head_ratio, 0)
        strengths = lax.dynamic_slice_in_dim(beta_gate, group_index * head_ratio, head_ratio, 0)

        def one_head(head_values, head_decay, head_beta):
            return run_head(queries.reshape(block_count, BLOCK, DK), key_rows.reshape(block_count, BLOCK, DK), head_values.reshape(block_count, BLOCK, DV), head_decay.reshape(block_count, BLOCK), head_beta.reshape(block_count, BLOCK))
        attended = jax.vmap(one_head)(values, decays, strengths)
        gate_cols = lax.dynamic_slice_in_dim(output_gate, group_index * head_ratio * DV, head_ratio * DV, 1)
        gate_values = jax.nn.silu(gate_cols.astype(jnp.float32)).reshape(TOKEN_POSITIONS, head_ratio, DV).transpose(1, 0, 2)
        scaled = attended * lax.rsqrt(lax.optimization_barrier(jnp.mean(attended * attended, axis=-1, keepdims=True)) + 1e-06)
        normed = scaled * norm_gain * gate_values
        return normed.transpose(1, 0, 2).reshape(TOKEN_POSITIONS, head_ratio * DV).astype(jnp.bfloat16)
    grouped = lax.map(group_out, jnp.arange(HK, dtype=jnp.int32))
    normed_all = grouped.transpose(1, 0, 2).reshape(TOKEN_POSITIONS, VCH)
    share_cols = VCH // N_TP
    summed = jnp.zeros((TOKEN_POSITIONS, DMODEL), jnp.float32)
    for tp_part in range(N_TP):
        partial_term = jnp.dot(normed_all[:, tp_part * share_cols:(tp_part + 1) * share_cols].astype(jnp.float32), out_weight[tp_part * share_cols:(tp_part + 1) * share_cols].astype(jnp.float32), preferred_element_type=jnp.float32)
        partial_term = lax.optimization_barrier(partial_term.astype(jnp.bfloat16)).astype(jnp.float32)
        summed = summed + partial_term
    return summed.astype(jnp.bfloat16)
```

```python
import jax
import jax.numpy as jnp
from jax import lax
from jax.sharding import PartitionSpec as P

VALUE_HEADS = 32
HK = 16
DK = 128
DV = 128
KCONV = 4
BLOCK = 64


exact_matmul_mode = lax.Precision.HIGHEST


def passed_along(block, axis, distance):
    devices = range(lax.axis_size(axis))
    route = [(i - distance, i) for i in devices if i - distance in devices]
    return lax.ppermute(block, axis, route)


def l2_rows(tensor):
    return tensor * lax.rsqrt(jnp.sum(tensor * tensor, axis=-1, keepdims=True) + 1e-06)


def matmul_heads(former, latter):
    return jnp.einsum("hij,hjk->hik", former, latter, precision=exact_matmul_mode)


def block_product(former, latter):
    return jnp.einsum("hnij,hnjk->hnik", former, latter, precision=exact_matmul_mode)


def unit_lower_inverse(system, identity_block):
    power = identity_block - system
    inverse = identity_block + power
    for squaring in range(5):
        power = block_product(power, power)
        inverse = inverse + block_product(inverse, power)
    return inverse


def body(qkv_input, conv_weight, log_decay, beta_gate, output_gate, norm_gain, out_weight):
    tokens = qkv_input.shape[0]
    head_ratio = VALUE_HEADS // HK
    group_width = 2 * DK + head_ratio * DV
    group_count = qkv_input.shape[1] // group_width
    head_count = group_count * head_ratio
    block_count = tokens // BLOCK
    last_rows = qkv_input[tokens - (KCONV - 1) :]
    prior_rows = passed_along(last_rows, "ctx", 1)
    padded = jnp.concatenate([prior_rows, qkv_input], 0).astype(jnp.float32)
    conv_taps = conv_weight.astype(jnp.float32)
    mixed = conv_taps[0] * padded[0:tokens]
    for offset in range(1, KCONV):
        mixed = mixed + conv_taps[offset] * padded[offset : offset + tokens]
    mixed = jax.nn.silu(mixed).reshape(tokens, group_count, group_width)
    queries = jnp.repeat(
        (l2_rows(mixed[:, :, :DK]) * DK ** (-0.5)).astype(jnp.bfloat16), head_ratio, axis=1
    )
    key_rows = jnp.repeat(
        l2_rows(mixed[:, :, DK : 2 * DK]).astype(jnp.bfloat16), head_ratio, axis=1
    )
    values = mixed[:, :, 2 * DK :].astype(jnp.bfloat16).reshape(tokens, head_count, DV)

    def blocked(tensor):
        return tensor.reshape(block_count, BLOCK, head_count, tensor.shape[-1]).transpose(
            2, 0, 1, 3
        )

    query_low = blocked(queries)
    key_low = blocked(key_rows)
    query_blocks = query_low.astype(jnp.float32)
    key_blocks = key_low.astype(jnp.float32)
    value_blocks = blocked(values).astype(jnp.float32)
    decay_blocks = log_decay.reshape(head_count, block_count, BLOCK)
    beta_blocks = beta_gate.reshape(head_count, block_count, BLOCK)
    position = jnp.arange(BLOCK)
    lower_mask = position[:, None] >= position[None, :]
    strict_mask = position[:, None] > position[None, :]
    identity_block = jnp.eye(BLOCK, dtype=jnp.float32)
    identity_key = jnp.eye(DK, dtype=jnp.float32)
    cumulative = jnp.cumsum(decay_blocks, axis=-1)
    exponent = jnp.where(lower_mask, cumulative[..., :, None] - cumulative[..., None, :], 0.0)
    damping = jnp.where(lower_mask, jnp.exp(exponent), 0.0)
    key_gram = jnp.einsum("hnik,hnjk->hnij", key_low, key_low, preferred_element_type=jnp.float32)
    system = identity_block + jnp.where(
        strict_mask, beta_blocks[..., :, None] * key_gram * damping, 0.0
    )
    inverse_system = unit_lower_inverse(system, identity_block)
    right_sides = jnp.concatenate(
        [
            beta_blocks[..., None] * value_blocks,
            (beta_blocks * jnp.exp(cumulative))[..., None] * key_blocks,
        ],
        -1,
    )
    solved = block_product(inverse_system, right_sides)
    fresh_values = solved[..., :DV]
    wy_weights = solved[..., DV:]
    scores = (
        jnp.einsum("hnik,hnjk->hnij", query_low, key_low, preferred_element_type=jnp.float32)
        * damping
    )
    query_decayed = jnp.exp(cumulative)[..., None] * query_blocks
    last_cum = cumulative[..., -1]
    key_decayed = jnp.exp(last_cum[..., None] - cumulative)[..., None] * key_blocks
    last_gain = jnp.exp(last_cum)
    block_trans = last_gain[..., None, None] * identity_key - jnp.einsum(
        "hnik,hnij->hnkj", key_decayed, wy_weights, precision=exact_matmul_mode
    )
    block_state = jnp.einsum(
        "hnik,hniv->hnkv", key_decayed, fresh_values, precision=exact_matmul_mode
    )

    lanes = lax.axis_size("tp")
    steps = block_count // lanes

    def compose(first, second):
        first_trans, first_state = first
        second_trans, second_state = second
        return (
            block_product(second_trans, first_trans),
            block_product(second_trans, first_state) + second_state,
        )

    level = (block_trans, block_state)
    while level[0].shape[1] > lanes:
        level = compose(
            (level[0][:, 0::2], level[1][:, 0::2]), (level[0][:, 1::2], level[1][:, 1::2])
        )
    lane_trans, lane_state = level
    while level[0].shape[1] > 1:
        level = compose(
            (level[0][:, 0::2], level[1][:, 0::2]), (level[0][:, 1::2], level[1][:, 1::2])
        )
    dev_trans, dev_state = level[0][:, 0], level[1][:, 0]
    zero_state = jnp.zeros((head_count, DK, DV), jnp.float32)

    def relay(turn_index, present_state):
        leaving = matmul_heads(dev_trans, present_state) + dev_state
        return passed_along(leaving.astype(jnp.bfloat16), "ctx", 1).astype(leaving.dtype)

    entering = lax.fori_loop(0, lax.axis_size("ctx") - 1, relay, zero_state)
    lane_entry = [entering]
    for lane in range(1, lanes):
        lane_entry.append(
            matmul_heads(lane_trans[:, lane - 1], lane_entry[-1]) + lane_state[:, lane - 1]
        )
    present_state = jnp.stack(lane_entry, 1)

    def by_step(tensor):
        return tensor.reshape((head_count, lanes, steps) + tensor.shape[2:])

    query_decayed = by_step(query_decayed)
    wy_weights = by_step(wy_weights)
    fresh_values = by_step(fresh_values)
    scores = by_step(scores)
    key_decayed = by_step(key_decayed)
    last_gain = by_step(last_gain)
    gate_values = jax.nn.silu(output_gate.astype(jnp.float32)).reshape(
        lanes, steps, BLOCK, head_count, DV
    )
    pieces = []
    for step in range(steps):
        updated_value_rows = fresh_values[:, :, step] - block_product(
            wy_weights[:, :, step], present_state
        )
        emitted = block_product(query_decayed[:, :, step], present_state) + block_product(
            scores[:, :, step], updated_value_rows
        )
        if step + 1 < steps:
            present_state = last_gain[:, :, step][..., None, None] * present_state + jnp.einsum(
                "hnpi,hnpj->hnij",
                key_decayed[:, :, step],
                updated_value_rows,
                precision=exact_matmul_mode,
            )
        attended = emitted.transpose(1, 2, 0, 3)
        scaled = attended * lax.rsqrt(jnp.mean(attended * attended, axis=-1, keepdims=True) + 1e-06)
        normed = (
            (scaled * norm_gain * gate_values[:, step])
            .astype(jnp.bfloat16)
            .reshape(lanes * BLOCK, head_count * DV)
        )
        pieces.append(
            lax.psum_scatter(
                jnp.dot(normed, out_weight, preferred_element_type=jnp.float32).astype(
                    jnp.bfloat16
                ),
                "tp",
                scatter_dimension=0,
                tiled=True,
            )
        )
    return jnp.concatenate(pieces, 0)


def solution(mesh):
    in_specs = (
        P("ctx", "tp"),
        P(None, "tp"),
        P("tp", "ctx"),
        P("tp", "ctx"),
        P("ctx", "tp"),
        P(),
        P("tp", None),
    )
    out_specs = P(("ctx", "tp"), None)
    return jax.shard_map(body, mesh=mesh, in_specs=in_specs, out_specs=out_specs, check_vma=False)
```

```python
import jax
import jax.numpy as jnp
from jax import lax
from jax.sharding import PartitionSpec as P

VALUE_HEADS = 32
HK = 16
DK = 128
DV = 128
KCONV = 4
BLOCK = 64


exact_matmul_mode = lax.Precision.HIGHEST


def passed_along(block, axis, distance):
    devices = range(lax.axis_size(axis))
    route = [(i - distance, i) for i in devices if i - distance in devices]
    return lax.ppermute(block, axis, route)


def l2_rows(tensor):
    return tensor * lax.rsqrt(jnp.sum(tensor * tensor, axis=-1, keepdims=True) + 1e-06)


def matmul_heads(former, latter):
    return jnp.einsum("hij,hjk->hik", former, latter, precision=exact_matmul_mode)


def block_product(former, latter):
    return jnp.einsum("hnij,hnjk->hnik", former, latter, precision=exact_matmul_mode)


def unit_lower_inverse(system, identity_block):
    power = identity_block - system
    inverse = identity_block + power
    for squaring in range(5):
        power = block_product(power, power)
        inverse = inverse + block_product(inverse, power)
    return inverse


def body(qkv_input, conv_weight, log_decay, beta_gate, output_gate, norm_gain, out_weight):
    tokens = qkv_input.shape[0]
    head_ratio = VALUE_HEADS // HK
    group_width = 2 * DK + head_ratio * DV
    group_count = qkv_input.shape[1] // group_width
    head_count = group_count * head_ratio
    block_count = tokens // BLOCK
    last_rows = qkv_input[tokens - (KCONV - 1) :]
    prior_rows = passed_along(last_rows, "ctx", 1)
    padded = jnp.concatenate([prior_rows, qkv_input], 0).astype(jnp.float32)
    conv_taps = conv_weight.astype(jnp.float32)
    mixed = conv_taps[0] * padded[0:tokens]
    for offset in range(1, KCONV):
        mixed = mixed + conv_taps[offset] * padded[offset : offset + tokens]
    mixed = jax.nn.silu(mixed).reshape(tokens, group_count, group_width)
    queries = jnp.repeat(
        (l2_rows(mixed[:, :, :DK]) * DK ** (-0.5)).astype(jnp.bfloat16), head_ratio, axis=1
    )
    key_rows = jnp.repeat(
        l2_rows(mixed[:, :, DK : 2 * DK]).astype(jnp.bfloat16), head_ratio, axis=1
    )
    values = mixed[:, :, 2 * DK :].astype(jnp.bfloat16).reshape(tokens, head_count, DV)

    def blocked(tensor):
        return tensor.reshape(block_count, BLOCK, head_count, tensor.shape[-1]).transpose(
            2, 0, 1, 3
        )

    query_low = blocked(queries)
    key_low = blocked(key_rows)
    query_blocks = query_low.astype(jnp.float32)
    key_blocks = key_low.astype(jnp.float32)
    value_blocks = blocked(values).astype(jnp.float32)
    decay_blocks = log_decay.reshape(head_count, block_count, BLOCK)
    beta_blocks = beta_gate.reshape(head_count, block_count, BLOCK)
    position = jnp.arange(BLOCK)
    lower_mask = position[:, None] >= position[None, :]
    strict_mask = position[:, None] > position[None, :]
    identity_block = jnp.eye(BLOCK, dtype=jnp.float32)
    identity_key = jnp.eye(DK, dtype=jnp.float32)
    cumulative = jnp.cumsum(decay_blocks, axis=-1)
    exponent = jnp.where(lower_mask, cumulative[..., :, None] - cumulative[..., None, :], 0.0)
    damping = jnp.where(lower_mask, jnp.exp(exponent), 0.0)
    key_gram = jnp.einsum("hnik,hnjk->hnij", key_low, key_low, preferred_element_type=jnp.float32)
    system = identity_block + jnp.where(
        strict_mask, beta_blocks[..., :, None] * key_gram * damping, 0.0
    )
    inverse_system = unit_lower_inverse(system, identity_block)
    right_sides = jnp.concatenate(
        [
            beta_blocks[..., None] * value_blocks,
            (beta_blocks * jnp.exp(cumulative))[..., None] * key_blocks,
        ],
        -1,
    )
    solved = block_product(inverse_system, right_sides)
    fresh_values = solved[..., :DV]
    wy_weights = solved[..., DV:]
    scores = (
        jnp.einsum("hnik,hnjk->hnij", query_low, key_low, preferred_element_type=jnp.float32)
        * damping
    )
    query_decayed = jnp.exp(cumulative)[..., None] * query_blocks
    last_cum = cumulative[..., -1]
    key_decayed = jnp.exp(last_cum[..., None] - cumulative)[..., None] * key_blocks
    last_gain = jnp.exp(last_cum)
    block_trans = last_gain[..., None, None] * identity_key - jnp.einsum(
        "hnik,hnij->hnkj", key_decayed, wy_weights, precision=exact_matmul_mode
    )
    block_state = jnp.einsum(
        "hnik,hniv->hnkv", key_decayed, fresh_values, precision=exact_matmul_mode
    )

    lanes = lax.axis_size("tp")
    steps = block_count // lanes

    def compose(first, second):
        first_trans, first_state = first
        second_trans, second_state = second
        return (
            block_product(second_trans, first_trans),
            block_product(second_trans, first_state) + second_state,
        )

    level = (block_trans, block_state)
    while level[0].shape[1] > lanes:
        level = compose(
            (level[0][:, 0::2], level[1][:, 0::2]), (level[0][:, 1::2], level[1][:, 1::2])
        )
    lane_trans, lane_state = level
    while level[0].shape[1] > 1:
        level = compose(
            (level[0][:, 0::2], level[1][:, 0::2]), (level[0][:, 1::2], level[1][:, 1::2])
        )
    dev_trans, dev_state = level[0][:, 0], level[1][:, 0]
    zero_state = jnp.zeros((head_count, DK, DV), jnp.float32)

    def relay(turn_index, present_state):
        leaving = matmul_heads(dev_trans, present_state) + dev_state
        return passed_along(leaving.astype(jnp.bfloat16), "ctx", 1).astype(leaving.dtype)

    entering = lax.fori_loop(0, lax.axis_size("ctx") - 1, relay, zero_state)
    lane_entry = [entering]
    for lane in range(1, lanes):
        lane_entry.append(
            matmul_heads(lane_trans[:, lane - 1], lane_entry[-1]) + lane_state[:, lane - 1]
        )
    present_state = jnp.stack(lane_entry, 1)

    def by_step(tensor):
        return tensor.reshape((head_count, lanes, steps) + tensor.shape[2:])

    query_decayed = by_step(query_decayed)
    wy_weights = by_step(wy_weights)
    fresh_values = by_step(fresh_values)
    scores = by_step(scores)
    key_decayed = by_step(key_decayed)
    last_gain = by_step(last_gain)
    gate_values = jax.nn.silu(output_gate.astype(jnp.float32)).reshape(
        lanes, steps, BLOCK, head_count, DV
    )
    tp_index = lax.axis_index("tp")

    def summed_share(partial):
        total = lax.dynamic_index_in_dim(partial, tp_index, 0, keepdims=False).astype(jnp.float32)
        for shift in range(1, lanes):
            outgoing = lax.dynamic_index_in_dim(partial, (tp_index + shift) % lanes, 0, keepdims=False)
            route = [(i, (i + shift) % lanes) for i in range(lanes)]
            total = total + lax.ppermute(outgoing, "tp", route).astype(jnp.float32)
        return total.astype(jnp.bfloat16)

    pieces = []
    for step in range(steps):
        updated_value_rows = fresh_values[:, :, step] - block_product(
            wy_weights[:, :, step], present_state
        )
        emitted = block_product(query_decayed[:, :, step], present_state) + block_product(
            scores[:, :, step], updated_value_rows
        )
        if step + 1 < steps:
            present_state = last_gain[:, :, step][..., None, None] * present_state + jnp.einsum(
                "hnpi,hnpj->hnij",
                key_decayed[:, :, step],
                updated_value_rows,
                precision=exact_matmul_mode,
            )
        attended = emitted.transpose(1, 2, 0, 3)
        scaled = attended * lax.rsqrt(jnp.mean(attended * attended, axis=-1, keepdims=True) + 1e-06)
        normed = (
            (scaled * norm_gain * gate_values[:, step])
            .astype(jnp.bfloat16)
            .reshape(lanes * BLOCK, head_count * DV)
        )
        pieces.append(
            summed_share(
                jnp.dot(normed, out_weight, preferred_element_type=jnp.float32)
                .astype(jnp.bfloat16)
                .reshape(lanes, BLOCK, -1)
            )
        )
    return jnp.concatenate(pieces, 0)


def solution(mesh):
    in_specs = (
        P("ctx", "tp"),
        P(None, "tp"),
        P("tp", "ctx"),
        P("tp", "ctx"),
        P("ctx", "tp"),
        P(),
        P("tp", None),
    )
    out_specs = P(("ctx", "tp"), None)
    return jax.shard_map(body, mesh=mesh, in_specs=in_specs, out_specs=out_specs, check_vma=False)
```

```python
import jax
import jax.numpy as jnp
from jax import lax
from jax.sharding import PartitionSpec as P

VALUE_HEADS = 32
HK = 16
DK = 128
DV = 128
KCONV = 4
BLOCK = 64


exact_matmul_mode = lax.Precision.HIGH


def passed_along(block, axis, distance):
    devices = range(lax.axis_size(axis))
    route = [(i - distance, i) for i in devices if i - distance in devices]
    return lax.ppermute(block, axis, route)


def l2_rows(tensor):
    return tensor * lax.rsqrt(jnp.sum(tensor * tensor, axis=-1, keepdims=True) + 1e-06)


def matmul_heads(former, latter):
    return jnp.einsum("hij,hjk->hik", former, latter, precision=exact_matmul_mode)


def block_product(former, latter):
    return jnp.einsum("hnij,hnjk->hnik", former, latter, precision=exact_matmul_mode)


def unit_lower_inverse(system, identity_block):
    power = identity_block - system
    inverse = identity_block + power
    for squaring in range(5):
        power = block_product(power, power)
        inverse = inverse + block_product(inverse, power)
    return inverse


def body(qkv_input, conv_weight, log_decay, beta_gate, output_gate, norm_gain, out_weight):
    tokens = qkv_input.shape[0]
    head_ratio = VALUE_HEADS // HK
    group_width = 2 * DK + head_ratio * DV
    group_count = qkv_input.shape[1] // group_width
    head_count = group_count * head_ratio
    block_count = tokens // BLOCK
    last_rows = qkv_input[tokens - (KCONV - 1) :]
    prior_rows = passed_along(last_rows, "ctx", 1)
    padded = jnp.concatenate([prior_rows, qkv_input], 0).astype(jnp.float32)
    conv_taps = conv_weight.astype(jnp.float32)
    mixed = conv_taps[0] * padded[0:tokens]
    for offset in range(1, KCONV):
        mixed = mixed + conv_taps[offset] * padded[offset : offset + tokens]
    mixed = jax.nn.silu(mixed).reshape(tokens, group_count, group_width)
    queries = jnp.repeat(
        (l2_rows(mixed[:, :, :DK]) * DK ** (-0.5)).astype(jnp.bfloat16), head_ratio, axis=1
    )
    key_rows = jnp.repeat(
        l2_rows(mixed[:, :, DK : 2 * DK]).astype(jnp.bfloat16), head_ratio, axis=1
    )
    values = mixed[:, :, 2 * DK :].astype(jnp.bfloat16).reshape(tokens, head_count, DV)

    def blocked(tensor):
        return tensor.reshape(block_count, BLOCK, head_count, tensor.shape[-1]).transpose(
            2, 0, 1, 3
        )

    query_low = blocked(queries)
    key_low = blocked(key_rows)
    query_blocks = query_low.astype(jnp.float32)
    key_blocks = key_low.astype(jnp.float32)
    value_blocks = blocked(values).astype(jnp.float32)
    decay_blocks = log_decay.reshape(head_count, block_count, BLOCK)
    beta_blocks = beta_gate.reshape(head_count, block_count, BLOCK)
    position = jnp.arange(BLOCK)
    lower_mask = position[:, None] >= position[None, :]
    strict_mask = position[:, None] > position[None, :]
    identity_block = jnp.eye(BLOCK, dtype=jnp.float32)
    identity_key = jnp.eye(DK, dtype=jnp.float32)
    cumulative = jnp.cumsum(decay_blocks, axis=-1)
    exponent = jnp.where(lower_mask, cumulative[..., :, None] - cumulative[..., None, :], 0.0)
    damping = jnp.where(lower_mask, jnp.exp(exponent), 0.0)
    key_gram = jnp.einsum("hnik,hnjk->hnij", key_low, key_low, preferred_element_type=jnp.float32)
    system = identity_block + jnp.where(
        strict_mask, beta_blocks[..., :, None] * key_gram * damping, 0.0
    )
    inverse_system = unit_lower_inverse(system, identity_block)
    right_sides = jnp.concatenate(
        [
            beta_blocks[..., None] * value_blocks,
            (beta_blocks * jnp.exp(cumulative))[..., None] * key_blocks,
        ],
        -1,
    )
    solved = block_product(inverse_system, right_sides)
    fresh_values = solved[..., :DV]
    wy_weights = solved[..., DV:]
    scores = (
        jnp.einsum("hnik,hnjk->hnij", query_low, key_low, preferred_element_type=jnp.float32)
        * damping
    )
    query_decayed = jnp.exp(cumulative)[..., None] * query_blocks
    last_cum = cumulative[..., -1]
    key_decayed = jnp.exp(last_cum[..., None] - cumulative)[..., None] * key_blocks
    last_gain = jnp.exp(last_cum)
    block_trans = last_gain[..., None, None] * identity_key - jnp.einsum(
        "hnik,hnij->hnkj", key_decayed, wy_weights, precision=exact_matmul_mode
    )
    block_state = jnp.einsum(
        "hnik,hniv->hnkv", key_decayed, fresh_values, precision=exact_matmul_mode
    )

    lanes = lax.axis_size("tp")
    steps = block_count // lanes

    def compose(first, second):
        first_trans, first_state = first
        second_trans, second_state = second
        return (
            block_product(second_trans, first_trans),
            block_product(second_trans, first_state) + second_state,
        )

    level = (block_trans, block_state)
    while level[0].shape[1] > lanes:
        level = compose(
            (level[0][:, 0::2], level[1][:, 0::2]), (level[0][:, 1::2], level[1][:, 1::2])
        )
    lane_trans, lane_state = level
    while level[0].shape[1] > 1:
        level = compose(
            (level[0][:, 0::2], level[1][:, 0::2]), (level[0][:, 1::2], level[1][:, 1::2])
        )
    dev_trans, dev_state = level[0][:, 0], level[1][:, 0]
    zero_state = jnp.zeros((head_count, DK, DV), jnp.float32)

    def relay(turn_index, present_state):
        leaving = matmul_heads(dev_trans, present_state) + dev_state
        return passed_along(leaving.astype(jnp.bfloat16), "ctx", 1).astype(leaving.dtype)

    entering = lax.fori_loop(0, lax.axis_size("ctx") - 1, relay, zero_state)
    lane_entry = [entering]
    for lane in range(1, lanes):
        lane_entry.append(
            matmul_heads(lane_trans[:, lane - 1], lane_entry[-1]) + lane_state[:, lane - 1]
        )
    present_state = jnp.stack(lane_entry, 1)

    def by_step(tensor):
        return tensor.reshape((head_count, lanes, steps) + tensor.shape[2:])

    query_decayed = by_step(query_decayed)
    wy_weights = by_step(wy_weights)
    fresh_values = by_step(fresh_values)
    scores = by_step(scores)
    key_decayed = by_step(key_decayed)
    last_gain = by_step(last_gain)
    gate_values = jax.nn.silu(output_gate.astype(jnp.float32)).reshape(
        lanes, steps, BLOCK, head_count, DV
    )
    tp_index = lax.axis_index("tp")

    def summed_share(partial):
        total = lax.dynamic_index_in_dim(partial, tp_index, 0, keepdims=False).astype(jnp.float32)
        for shift in range(1, lanes):
            outgoing = lax.dynamic_index_in_dim(partial, (tp_index + shift) % lanes, 0, keepdims=False)
            route = [(i, (i + shift) % lanes) for i in range(lanes)]
            total = total + lax.ppermute(outgoing, "tp", route).astype(jnp.float32)
        return total.astype(jnp.bfloat16)

    pieces = []
    for step in range(steps):
        updated_value_rows = fresh_values[:, :, step] - block_product(
            wy_weights[:, :, step], present_state
        )
        emitted = block_product(query_decayed[:, :, step], present_state) + block_product(
            scores[:, :, step], updated_value_rows
        )
        if step + 1 < steps:
            present_state = last_gain[:, :, step][..., None, None] * present_state + jnp.einsum(
                "hnpi,hnpj->hnij",
                key_decayed[:, :, step],
                updated_value_rows,
                precision=exact_matmul_mode,
            )
        attended = emitted.transpose(1, 2, 0, 3)
        scaled = attended * lax.rsqrt(jnp.mean(attended * attended, axis=-1, keepdims=True) + 1e-06)
        normed = (
            (scaled * norm_gain * gate_values[:, step])
            .astype(jnp.bfloat16)
            .reshape(lanes * BLOCK, head_count * DV)
        )
        pieces.append(
            summed_share(
                jnp.dot(normed, out_weight, preferred_element_type=jnp.float32)
                .astype(jnp.bfloat16)
                .reshape(lanes, BLOCK, -1)
            )
        )
    return jnp.concatenate(pieces, 0)


def solution(mesh):
    in_specs = (
        P("ctx", "tp"),
        P(None, "tp"),
        P("tp", "ctx"),
        P("tp", "ctx"),
        P("ctx", "tp"),
        P(),
        P("tp", None),
    )
    out_specs = P(("ctx", "tp"), None)
    return jax.shard_map(body, mesh=mesh, in_specs=in_specs, out_specs=out_specs, check_vma=False)
```

```python
import jax
import jax.numpy as jnp
from jax import lax
from jax.sharding import PartitionSpec as P

VALUE_HEADS = 32
HK = 16
DK = 128
DV = 128
KCONV = 4
BLOCK = 64


exact_matmul_mode = lax.Precision.HIGH


def passed_along(block, axis, distance):
    devices = range(lax.axis_size(axis))
    route = [(i - distance, i) for i in devices if i - distance in devices]
    return lax.ppermute(block, axis, route)


def l2_rows(tensor):
    return tensor * lax.rsqrt(jnp.sum(tensor * tensor, axis=-1, keepdims=True) + 1e-06)


def matmul_heads(former, latter):
    return jnp.einsum("hij,hjk->hik", former, latter, precision=exact_matmul_mode)


def block_product(former, latter):
    return jnp.einsum("hnij,hnjk->hnik", former, latter, precision=exact_matmul_mode)


def unit_lower_inverse(system, identity_block):
    power = identity_block - system
    inverse = identity_block + power
    for squaring in range(5):
        power = block_product(power, power)
        inverse = inverse + block_product(inverse, power)
    return inverse


def body(qkv_input, conv_weight, log_decay, beta_gate, output_gate, norm_gain, out_weight):
    tokens = qkv_input.shape[0]
    head_ratio = VALUE_HEADS // HK
    group_width = 2 * DK + head_ratio * DV
    group_count = qkv_input.shape[1] // group_width
    head_count = group_count * head_ratio
    block_count = tokens // BLOCK
    last_rows = qkv_input[tokens - (KCONV - 1) :]
    prior_rows = passed_along(last_rows, "ctx", 1)
    padded = jnp.concatenate([prior_rows, qkv_input], 0).astype(jnp.float32)
    conv_taps = conv_weight.astype(jnp.float32)
    mixed = conv_taps[0] * padded[0:tokens]
    for offset in range(1, KCONV):
        mixed = mixed + conv_taps[offset] * padded[offset : offset + tokens]
    mixed = jax.nn.silu(mixed).reshape(tokens, group_count, group_width)
    queries = jnp.repeat(
        (l2_rows(mixed[:, :, :DK]) * DK ** (-0.5)).astype(jnp.bfloat16), head_ratio, axis=1
    )
    key_rows = jnp.repeat(
        l2_rows(mixed[:, :, DK : 2 * DK]).astype(jnp.bfloat16), head_ratio, axis=1
    )
    values = mixed[:, :, 2 * DK :].astype(jnp.bfloat16).reshape(tokens, head_count, DV)

    def blocked(tensor):
        return tensor.reshape(block_count, BLOCK, head_count, tensor.shape[-1]).transpose(
            2, 0, 1, 3
        )

    query_low = blocked(queries)
    key_low = blocked(key_rows)
    query_blocks = query_low.astype(jnp.float32)
    key_blocks = key_low.astype(jnp.float32)
    value_blocks = blocked(values).astype(jnp.float32)
    decay_blocks = log_decay.reshape(head_count, block_count, BLOCK)
    beta_blocks = beta_gate.reshape(head_count, block_count, BLOCK)
    position = jnp.arange(BLOCK)
    lower_mask = position[:, None] >= position[None, :]
    strict_mask = position[:, None] > position[None, :]
    identity_block = jnp.eye(BLOCK, dtype=jnp.float32)
    identity_key = jnp.eye(DK, dtype=jnp.float32)
    cumulative = jnp.cumsum(decay_blocks, axis=-1)
    exponent = jnp.where(lower_mask, cumulative[..., :, None] - cumulative[..., None, :], 0.0)
    damping = jnp.where(lower_mask, jnp.exp(exponent), 0.0)
    key_gram = jnp.einsum("hnik,hnjk->hnij", key_low, key_low, preferred_element_type=jnp.float32)
    system = identity_block + jnp.where(
        strict_mask, beta_blocks[..., :, None] * key_gram * damping, 0.0
    )
    inverse_system = unit_lower_inverse(system, identity_block)
    right_sides = jnp.concatenate(
        [
            beta_blocks[..., None] * value_blocks,
            (beta_blocks * jnp.exp(cumulative))[..., None] * key_blocks,
        ],
        -1,
    )
    solved = block_product(inverse_system, right_sides)
    fresh_values = solved[..., :DV]
    wy_weights = solved[..., DV:]
    scores = (
        jnp.einsum("hnik,hnjk->hnij", query_low, key_low, preferred_element_type=jnp.float32)
        * damping
    )
    query_decayed = jnp.exp(cumulative)[..., None] * query_blocks
    last_cum = cumulative[..., -1]
    key_decayed = jnp.exp(last_cum[..., None] - cumulative)[..., None] * key_blocks
    last_gain = jnp.exp(last_cum)
    block_trans = last_gain[..., None, None] * identity_key - jnp.einsum(
        "hnik,hnij->hnkj", key_decayed, wy_weights, precision=exact_matmul_mode
    )
    block_state = jnp.einsum(
        "hnik,hniv->hnkv", key_decayed, fresh_values, precision=exact_matmul_mode
    )

    lanes = lax.axis_size("tp")
    steps = block_count // lanes

    def compose(first, second):
        first_trans, first_state = first
        second_trans, second_state = second
        return (
            block_product(second_trans, first_trans),
            block_product(second_trans, first_state) + second_state,
        )

    level = (block_trans, block_state)
    while level[0].shape[1] > lanes:
        level = compose(
            (level[0][:, 0::2], level[1][:, 0::2]), (level[0][:, 1::2], level[1][:, 1::2])
        )
    lane_trans, lane_state = level
    while level[0].shape[1] > 1:
        level = compose(
            (level[0][:, 0::2], level[1][:, 0::2]), (level[0][:, 1::2], level[1][:, 1::2])
        )
    dev_trans, dev_state = level[0][:, 0], level[1][:, 0]
    zero_state = jnp.zeros((head_count, DK, DV), jnp.float32)

    def relay(turn_index, present_state):
        leaving = matmul_heads(dev_trans, present_state) + dev_state
        return passed_along(leaving.astype(jnp.bfloat16), "ctx", 1).astype(leaving.dtype)

    entering = lax.fori_loop(0, lax.axis_size("ctx") - 1, relay, zero_state)
    lane_entry = [entering]
    for lane in range(1, lanes):
        lane_entry.append(
            matmul_heads(lane_trans[:, lane - 1], lane_entry[-1]) + lane_state[:, lane - 1]
        )
    present_state = jnp.stack(lane_entry, 1)

    def by_step(tensor):
        return tensor.reshape((head_count, lanes, steps) + tensor.shape[2:])

    query_decayed = by_step(query_decayed)
    wy_weights = by_step(wy_weights)
    fresh_values = by_step(fresh_values)
    scores = by_step(scores)
    key_decayed = by_step(key_decayed)
    last_gain = by_step(last_gain)
    gate_values = jax.nn.silu(output_gate.astype(jnp.float32)).reshape(
        lanes, steps, BLOCK, head_count, DV
    )
    tp_index = lax.axis_index("tp")

    def summed_share(partial):
        total = lax.dynamic_index_in_dim(partial, tp_index, 0, keepdims=False).astype(jnp.float32)
        for direction in (1, -1):
            carried = None
            for stage in range(1, lanes):
                target = jnp.clip(tp_index + direction * (lanes - stage), 0, lanes - 1)
                outgoing = lax.dynamic_index_in_dim(partial, target, 0, keepdims=False)
                if carried is not None:
                    outgoing = (outgoing.astype(jnp.float32) + carried.astype(jnp.float32)).astype(
                        jnp.bfloat16
                    )
                if direction == 1:
                    route = [(i, i + 1) for i in range(stage)]
                else:
                    route = [(i, i - 1) for i in range(lanes - stage, lanes)]
                carried = lax.ppermute(outgoing, "tp", route)
            total = total + carried.astype(jnp.float32)
        return total.astype(jnp.bfloat16)

    pieces = []
    for step in range(steps):
        updated_value_rows = fresh_values[:, :, step] - block_product(
            wy_weights[:, :, step], present_state
        )
        emitted = block_product(query_decayed[:, :, step], present_state) + block_product(
            scores[:, :, step], updated_value_rows
        )
        if step + 1 < steps:
            present_state = last_gain[:, :, step][..., None, None] * present_state + jnp.einsum(
                "hnpi,hnpj->hnij",
                key_decayed[:, :, step],
                updated_value_rows,
                precision=exact_matmul_mode,
            )
        attended = emitted.transpose(1, 2, 0, 3)
        scaled = attended * lax.rsqrt(jnp.mean(attended * attended, axis=-1, keepdims=True) + 1e-06)
        normed = (
            (scaled * norm_gain * gate_values[:, step])
            .astype(jnp.bfloat16)
            .reshape(lanes * BLOCK, head_count * DV)
        )
        partial = (
            jnp.dot(normed, out_weight, preferred_element_type=jnp.float32)
            .astype(jnp.bfloat16)
            .reshape(lanes, BLOCK, -1)
        )
        if step + 1 < steps:
            present_state, partial = lax.optimization_barrier((present_state, partial))
        pieces.append(summed_share(partial))
    return jnp.concatenate(pieces, 0)


def solution(mesh):
    in_specs = (
        P("ctx", "tp"),
        P(None, "tp"),
        P("tp", "ctx"),
        P("tp", "ctx"),
        P("ctx", "tp"),
        P(),
        P("tp", None),
    )
    out_specs = P(("ctx", "tp"), None)
    return jax.shard_map(body, mesh=mesh, in_specs=in_specs, out_specs=out_specs, check_vma=False)
```

```python
import jax
import jax.numpy as jnp
from jax import lax
from jax.sharding import PartitionSpec as P

VALUE_HEADS = 32
HK = 16
DK = 128
DV = 128
KCONV = 4
BLOCK = 64


exact_matmul_mode = lax.Precision.HIGH


def passed_along(block, axis, distance):
    devices = range(lax.axis_size(axis))
    route = [(i - distance, i) for i in devices if i - distance in devices]
    return lax.ppermute(block, axis, route)


def l2_rows(tensor):
    return tensor * lax.rsqrt(jnp.sum(tensor * tensor, axis=-1, keepdims=True) + 1e-06)


def matmul_heads(former, latter):
    return jnp.einsum("hij,hjk->hik", former, latter, precision=exact_matmul_mode)


def block_product(former, latter):
    return jnp.einsum("hnij,hnjk->hnik", former, latter, precision=exact_matmul_mode)


def unit_lower_inverse(system, identity_block):
    power = identity_block - system
    inverse = identity_block + power
    for squaring in range(5):
        power = block_product(power, power)
        inverse = inverse + block_product(inverse, power)
    return inverse


def body(qkv_input, conv_weight, log_decay, beta_gate, output_gate, norm_gain, out_weight):
    tokens = qkv_input.shape[0]
    head_ratio = VALUE_HEADS // HK
    group_width = 2 * DK + head_ratio * DV
    group_count = qkv_input.shape[1] // group_width
    head_count = group_count * head_ratio
    block_count = tokens // BLOCK
    last_rows = qkv_input[tokens - (KCONV - 1) :]
    prior_rows = passed_along(last_rows, "ctx", 1)
    padded = jnp.concatenate([prior_rows, qkv_input], 0).astype(jnp.float32)
    conv_taps = conv_weight.astype(jnp.float32)
    mixed = conv_taps[0] * padded[0:tokens]
    for offset in range(1, KCONV):
        mixed = mixed + conv_taps[offset] * padded[offset : offset + tokens]
    mixed = jax.nn.silu(mixed).reshape(tokens, group_count, group_width)
    queries = jnp.repeat(
        (l2_rows(mixed[:, :, :DK]) * DK ** (-0.5)).astype(jnp.bfloat16), head_ratio, axis=1
    )
    key_rows = jnp.repeat(
        l2_rows(mixed[:, :, DK : 2 * DK]).astype(jnp.bfloat16), head_ratio, axis=1
    )
    values = mixed[:, :, 2 * DK :].astype(jnp.bfloat16).reshape(tokens, head_count, DV)

    def blocked(tensor):
        return tensor.reshape(block_count, BLOCK, head_count, tensor.shape[-1]).transpose(
            2, 0, 1, 3
        )

    query_low = blocked(queries)
    key_low = blocked(key_rows)
    query_blocks = query_low.astype(jnp.float32)
    key_blocks = key_low.astype(jnp.float32)
    value_blocks = blocked(values).astype(jnp.float32)
    decay_blocks = log_decay.reshape(head_count, block_count, BLOCK)
    beta_blocks = beta_gate.reshape(head_count, block_count, BLOCK)
    position = jnp.arange(BLOCK)
    lower_mask = position[:, None] >= position[None, :]
    strict_mask = position[:, None] > position[None, :]
    identity_block = jnp.eye(BLOCK, dtype=jnp.float32)
    identity_key = jnp.eye(DK, dtype=jnp.float32)
    cumulative = jnp.cumsum(decay_blocks, axis=-1)
    exponent = jnp.where(lower_mask, cumulative[..., :, None] - cumulative[..., None, :], 0.0)
    damping = jnp.where(lower_mask, jnp.exp(exponent), 0.0)
    key_gram = jnp.einsum("hnik,hnjk->hnij", key_low, key_low, preferred_element_type=jnp.float32)
    system = identity_block + jnp.where(
        strict_mask, beta_blocks[..., :, None] * key_gram * damping, 0.0
    )
    inverse_system = unit_lower_inverse(system, identity_block)
    right_sides = jnp.concatenate(
        [
            beta_blocks[..., None] * value_blocks,
            (beta_blocks * jnp.exp(cumulative))[..., None] * key_blocks,
        ],
        -1,
    )
    solved = block_product(inverse_system, right_sides)
    fresh_values = solved[..., :DV]
    wy_weights = solved[..., DV:]
    scores = (
        jnp.einsum("hnik,hnjk->hnij", query_low, key_low, preferred_element_type=jnp.float32)
        * damping
    )
    query_decayed = jnp.exp(cumulative)[..., None] * query_blocks
    last_cum = cumulative[..., -1]
    key_decayed = jnp.exp(last_cum[..., None] - cumulative)[..., None] * key_blocks
    last_gain = jnp.exp(last_cum)
    block_trans = last_gain[..., None, None] * identity_key - jnp.einsum(
        "hnik,hnij->hnkj", key_decayed, wy_weights, precision=exact_matmul_mode
    )
    block_state = jnp.einsum(
        "hnik,hniv->hnkv", key_decayed, fresh_values, precision=exact_matmul_mode
    )

    lanes = lax.axis_size("tp")
    steps = block_count // lanes

    def compose(first, second):
        first_trans, first_state = first
        second_trans, second_state = second
        return (
            block_product(second_trans, first_trans),
            block_product(second_trans, first_state) + second_state,
        )

    level = (block_trans, block_state)
    while level[0].shape[1] > lanes:
        level = compose(
            (level[0][:, 0::2], level[1][:, 0::2]), (level[0][:, 1::2], level[1][:, 1::2])
        )
    lane_trans, lane_state = level
    while level[0].shape[1] > 1:
        level = compose(
            (level[0][:, 0::2], level[1][:, 0::2]), (level[0][:, 1::2], level[1][:, 1::2])
        )
    dev_trans, dev_state = level[0][:, 0], level[1][:, 0]
    zero_state = jnp.zeros((head_count, DK, DV), jnp.float32)

    def relay(turn_index, present_state):
        leaving = (matmul_heads(dev_trans, present_state) + dev_state).astype(jnp.bfloat16)
        parts = jnp.split(leaving, lanes, axis=0)
        return jnp.concatenate([passed_along(part, "ctx", 1) for part in parts], 0).astype(
            jnp.float32
        )

    entering = lax.fori_loop(0, lax.axis_size("ctx") - 1, relay, zero_state)
    lane_entry = [entering]
    for lane in range(1, lanes):
        lane_entry.append(
            matmul_heads(lane_trans[:, lane - 1], lane_entry[-1]) + lane_state[:, lane - 1]
        )
    present_state = jnp.stack(lane_entry, 1)

    def by_step(tensor):
        return tensor.reshape((head_count, lanes, steps) + tensor.shape[2:])

    query_decayed = by_step(query_decayed)
    wy_weights = by_step(wy_weights)
    fresh_values = by_step(fresh_values)
    scores = by_step(scores)
    key_decayed = by_step(key_decayed)
    last_gain = by_step(last_gain)
    gate_values = jax.nn.silu(output_gate.astype(jnp.float32)).reshape(
        lanes, steps, BLOCK, head_count, DV
    )
    tp_index = lax.axis_index("tp")

    def summed_share(partial):
        total = lax.dynamic_index_in_dim(partial, tp_index, 0, keepdims=False).astype(jnp.float32)
        for direction in (1, -1):
            carried = None
            for stage in range(1, lanes):
                target = jnp.clip(tp_index + direction * (lanes - stage), 0, lanes - 1)
                outgoing = lax.dynamic_index_in_dim(partial, target, 0, keepdims=False)
                if carried is not None:
                    outgoing = (outgoing.astype(jnp.float32) + carried.astype(jnp.float32)).astype(
                        jnp.bfloat16
                    )
                if direction == 1:
                    route = [(i, i + 1) for i in range(stage)]
                else:
                    route = [(i, i - 1) for i in range(lanes - stage, lanes)]
                carried = lax.ppermute(outgoing, "tp", route)
            total = total + carried.astype(jnp.float32)
        return total.astype(jnp.bfloat16)

    pieces = []
    for step in range(steps):
        updated_value_rows = fresh_values[:, :, step] - block_product(
            wy_weights[:, :, step], present_state
        )
        emitted = block_product(query_decayed[:, :, step], present_state) + block_product(
            scores[:, :, step], updated_value_rows
        )
        if step + 1 < steps:
            present_state = last_gain[:, :, step][..., None, None] * present_state + jnp.einsum(
                "hnpi,hnpj->hnij",
                key_decayed[:, :, step],
                updated_value_rows,
                precision=exact_matmul_mode,
            )
        attended = emitted.transpose(1, 2, 0, 3)
        scaled = attended * lax.rsqrt(jnp.mean(attended * attended, axis=-1, keepdims=True) + 1e-06)
        normed = (
            (scaled * norm_gain * gate_values[:, step])
            .astype(jnp.bfloat16)
            .reshape(lanes * BLOCK, head_count * DV)
        )
        partial = (
            jnp.dot(normed, out_weight, preferred_element_type=jnp.float32)
            .astype(jnp.bfloat16)
            .reshape(lanes, BLOCK, -1)
        )
        if step + 1 < steps:
            present_state, partial = lax.optimization_barrier((present_state, partial))
        pieces.append(summed_share(partial))
    return jnp.concatenate(pieces, 0)


def solution(mesh):
    in_specs = (
        P("ctx", "tp"),
        P(None, "tp"),
        P("tp", "ctx"),
        P("tp", "ctx"),
        P("ctx", "tp"),
        P(),
        P("tp", None),
    )
    out_specs = P(("ctx", "tp"), None)
    return jax.shard_map(body, mesh=mesh, in_specs=in_specs, out_specs=out_specs, check_vma=False)
```

```python
import jax
import jax.numpy as jnp
from jax import lax
from jax.sharding import PartitionSpec as P

VALUE_HEADS = 32
HK = 16
DK = 128
DV = 128
KCONV = 4
BLOCK = 64


exact_matmul_mode = lax.Precision.HIGH


def passed_along(block, axis, distance):
    devices = range(lax.axis_size(axis))
    route = [(i - distance, i) for i in devices if i - distance in devices]
    return lax.ppermute(block, axis, route)


def l2_rows(tensor):
    return tensor * lax.rsqrt(jnp.sum(tensor * tensor, axis=-1, keepdims=True) + 1e-06)


def matmul_heads(former, latter):
    return jnp.einsum("hij,hjk->hik", former, latter, precision=exact_matmul_mode)


def block_product(former, latter):
    return jnp.einsum("hnij,hnjk->hnik", former, latter, precision=exact_matmul_mode)


def unit_lower_inverse(system, identity_block):
    power = identity_block - system
    inverse = identity_block + power
    for squaring in range(5):
        power = block_product(power, power)
        inverse = inverse + block_product(inverse, power)
    return inverse


def body(qkv_input, conv_weight, log_decay, beta_gate, output_gate, norm_gain, out_weight):
    tokens = qkv_input.shape[0]
    head_ratio = VALUE_HEADS // HK
    group_width = 2 * DK + head_ratio * DV
    group_count = qkv_input.shape[1] // group_width
    head_count = group_count * head_ratio
    block_count = tokens // BLOCK
    last_rows = qkv_input[tokens - (KCONV - 1) :]
    prior_rows = passed_along(last_rows, "ctx", 1)
    padded = jnp.concatenate([prior_rows, qkv_input], 0).astype(jnp.float32)
    conv_taps = conv_weight.astype(jnp.float32)
    mixed = conv_taps[0] * padded[0:tokens]
    for offset in range(1, KCONV):
        mixed = mixed + conv_taps[offset] * padded[offset : offset + tokens]
    grouped = (
        jax.nn.silu(mixed)
        .reshape(block_count, BLOCK, group_count, group_width)
        .transpose(2, 0, 1, 3)
    )
    query_group = (l2_rows(grouped[..., :DK]) * DK ** (-0.5)).astype(jnp.bfloat16)
    key_group = l2_rows(grouped[..., DK : 2 * DK]).astype(jnp.bfloat16)
    value_low = (
        grouped[..., 2 * DK :]
        .astype(jnp.bfloat16)
        .reshape(group_count, block_count, BLOCK, head_ratio, DV)
        .transpose(0, 3, 1, 2, 4)
        .reshape(head_count, block_count, BLOCK, DV)
    )

    def per_head(tensor):
        return jnp.repeat(tensor, head_ratio, axis=0)

    query_low = per_head(query_group)
    key_low = per_head(key_group)
    query_blocks = query_low.astype(jnp.float32)
    key_blocks = key_low.astype(jnp.float32)
    value_blocks = value_low.astype(jnp.float32)
    decay_blocks = log_decay.reshape(head_count, block_count, BLOCK)
    beta_blocks = beta_gate.reshape(head_count, block_count, BLOCK)
    position = jnp.arange(BLOCK)
    lower_mask = position[:, None] >= position[None, :]
    strict_mask = position[:, None] > position[None, :]
    identity_block = jnp.eye(BLOCK, dtype=jnp.float32)
    identity_key = jnp.eye(DK, dtype=jnp.float32)
    cumulative = jnp.cumsum(decay_blocks, axis=-1)
    exponent = jnp.where(lower_mask, cumulative[..., :, None] - cumulative[..., None, :], 0.0)
    damping = jnp.where(lower_mask, jnp.exp(exponent), 0.0)
    key_gram = per_head(
        jnp.einsum("gnik,gnjk->gnij", key_group, key_group, preferred_element_type=jnp.float32)
    )
    system = identity_block + jnp.where(
        strict_mask, beta_blocks[..., :, None] * key_gram * damping, 0.0
    )
    inverse_system = unit_lower_inverse(system, identity_block)
    right_sides = jnp.concatenate(
        [
            beta_blocks[..., None] * value_blocks,
            (beta_blocks * jnp.exp(cumulative))[..., None] * key_blocks,
        ],
        -1,
    )
    solved = block_product(inverse_system, right_sides)
    fresh_values = solved[..., :DV]
    wy_weights = solved[..., DV:]
    scores = (
        per_head(
            jnp.einsum(
                "gnik,gnjk->gnij", query_group, key_group, preferred_element_type=jnp.float32
            )
        )
        * damping
    )
    query_decayed = jnp.exp(cumulative)[..., None] * query_blocks
    last_cum = cumulative[..., -1]
    key_decayed = jnp.exp(last_cum[..., None] - cumulative)[..., None] * key_blocks
    last_gain = jnp.exp(last_cum)
    block_trans = last_gain[..., None, None] * identity_key - jnp.einsum(
        "hnik,hnij->hnkj", key_decayed, wy_weights, precision=exact_matmul_mode
    )
    block_state = jnp.einsum(
        "hnik,hniv->hnkv", key_decayed, fresh_values, precision=exact_matmul_mode
    )

    lanes = lax.axis_size("tp")
    steps = block_count // lanes

    def compose(first, second):
        first_trans, first_state = first
        second_trans, second_state = second
        return (
            block_product(second_trans, first_trans),
            block_product(second_trans, first_state) + second_state,
        )

    level = (block_trans, block_state)
    while level[0].shape[1] > lanes:
        level = compose(
            (level[0][:, 0::2], level[1][:, 0::2]), (level[0][:, 1::2], level[1][:, 1::2])
        )
    lane_trans, lane_state = level
    while level[0].shape[1] > 1:
        level = compose(
            (level[0][:, 0::2], level[1][:, 0::2]), (level[0][:, 1::2], level[1][:, 1::2])
        )
    dev_trans, dev_state = level[0][:, 0], level[1][:, 0]
    zero_state = jnp.zeros((head_count, DK, DV), jnp.float32)

    def relay(turn_index, present_state):
        leaving = matmul_heads(dev_trans, present_state) + dev_state
        return passed_along(leaving.astype(jnp.bfloat16), "ctx", 1).astype(leaving.dtype)

    entering = lax.fori_loop(0, lax.axis_size("ctx") - 1, relay, zero_state)
    lane_entry = [entering]
    for lane in range(1, lanes):
        lane_entry.append(
            matmul_heads(lane_trans[:, lane - 1], lane_entry[-1]) + lane_state[:, lane - 1]
        )
    present_state = jnp.stack(lane_entry, 1)

    def by_step(tensor):
        return tensor.reshape((head_count, lanes, steps) + tensor.shape[2:])

    query_decayed = by_step(query_decayed)
    wy_weights = by_step(wy_weights)
    fresh_values = by_step(fresh_values)
    scores = by_step(scores)
    key_decayed = by_step(key_decayed)
    last_gain = by_step(last_gain)
    gate_values = jax.nn.silu(output_gate.astype(jnp.float32)).reshape(
        lanes, steps, BLOCK, head_count, DV
    )
    tp_index = lax.axis_index("tp")

    def summed_share(partial):
        total = lax.dynamic_index_in_dim(partial, tp_index, 0, keepdims=False).astype(jnp.float32)
        for direction in (1, -1):
            carried = None
            for stage in range(1, lanes):
                target = jnp.clip(tp_index + direction * (lanes - stage), 0, lanes - 1)
                outgoing = lax.dynamic_index_in_dim(partial, target, 0, keepdims=False)
                if carried is not None:
                    outgoing = (outgoing.astype(jnp.float32) + carried.astype(jnp.float32)).astype(
                        jnp.bfloat16
                    )
                if direction == 1:
                    route = [(i, i + 1) for i in range(stage)]
                else:
                    route = [(i, i - 1) for i in range(lanes - stage, lanes)]
                carried = lax.ppermute(outgoing, "tp", route)
            total = total + carried.astype(jnp.float32)
        return total.astype(jnp.bfloat16)

    pieces = []
    for step in range(steps):
        updated_value_rows = fresh_values[:, :, step] - block_product(
            wy_weights[:, :, step], present_state
        )
        emitted = block_product(query_decayed[:, :, step], present_state) + block_product(
            scores[:, :, step], updated_value_rows
        )
        if step + 1 < steps:
            present_state = last_gain[:, :, step][..., None, None] * present_state + jnp.einsum(
                "hnpi,hnpj->hnij",
                key_decayed[:, :, step],
                updated_value_rows,
                precision=exact_matmul_mode,
            )
        attended = emitted.transpose(1, 2, 0, 3)
        scaled = attended * lax.rsqrt(jnp.mean(attended * attended, axis=-1, keepdims=True) + 1e-06)
        normed = (
            (scaled * norm_gain * gate_values[:, step])
            .astype(jnp.bfloat16)
            .reshape(lanes * BLOCK, head_count * DV)
        )
        partial = (
            jnp.dot(normed, out_weight, preferred_element_type=jnp.float32)
            .astype(jnp.bfloat16)
            .reshape(lanes, BLOCK, -1)
        )
        if step + 1 < steps:
            present_state, partial = lax.optimization_barrier((present_state, partial))
        pieces.append(summed_share(partial))
    return jnp.concatenate(pieces, 0)


def solution(mesh):
    in_specs = (
        P("ctx", "tp"),
        P(None, "tp"),
        P("tp", "ctx"),
        P("tp", "ctx"),
        P("ctx", "tp"),
        P(),
        P("tp", None),
    )
    out_specs = P(("ctx", "tp"), None)
    return jax.shard_map(body, mesh=mesh, in_specs=in_specs, out_specs=out_specs, check_vma=False)
```

```python
import jax
import jax.numpy as jnp
from jax import lax
from jax.sharding import PartitionSpec as P

VALUE_HEADS = 32
HK = 16
DK = 128
DV = 128
KCONV = 4
BLOCK = 64


exact_matmul_mode = lax.Precision.HIGH


def passed_along(block, axis, distance):
    devices = range(lax.axis_size(axis))
    route = [(i - distance, i) for i in devices if i - distance in devices]
    return lax.ppermute(block, axis, route)


def l2_rows(tensor):
    return tensor * lax.rsqrt(jnp.sum(tensor * tensor, axis=-1, keepdims=True) + 1e-06)


def matmul_heads(former, latter):
    return jnp.einsum("hij,hjk->hik", former, latter, precision=exact_matmul_mode)


def block_product(former, latter):
    return jnp.einsum("hnij,hnjk->hnik", former, latter, precision=exact_matmul_mode)


def unit_lower_inverse(system, identity_block):
    power = identity_block - system
    inverse = identity_block + power
    for squaring in range(5):
        power = block_product(power, power)
        inverse = inverse + block_product(inverse, power)
    return inverse


def body(qkv_input, conv_weight, log_decay, beta_gate, output_gate, norm_gain, out_weight):
    tokens = qkv_input.shape[0]
    head_ratio = VALUE_HEADS // HK
    group_width = 2 * DK + head_ratio * DV
    group_count = qkv_input.shape[1] // group_width
    head_count = group_count * head_ratio
    block_count = tokens // BLOCK
    last_rows = qkv_input[tokens - (KCONV - 1) :]
    prior_rows = passed_along(last_rows, "ctx", 1)
    padded = jnp.concatenate([prior_rows, qkv_input], 0).astype(jnp.float32)
    conv_taps = conv_weight.astype(jnp.float32)
    mixed = conv_taps[0] * padded[0:tokens]
    for offset in range(1, KCONV):
        mixed = mixed + conv_taps[offset] * padded[offset : offset + tokens]
    activated = jax.nn.silu(mixed)

    def columns(starts, width):
        return jnp.stack([activated[:, start : start + width] for start in starts], 0).reshape(
            len(starts), block_count, BLOCK, width
        )

    group_starts = [group * group_width for group in range(group_count)]
    query_group = (l2_rows(columns(group_starts, DK)) * DK ** (-0.5)).astype(jnp.bfloat16)
    key_group = l2_rows(columns([start + DK for start in group_starts], DK)).astype(jnp.bfloat16)
    value_low = columns(
        [start + 2 * DK + part * DV for start in group_starts for part in range(head_ratio)], DV
    ).astype(jnp.bfloat16)

    def per_head(tensor):
        return jnp.repeat(tensor, head_ratio, axis=0)

    query_low = per_head(query_group)
    key_low = per_head(key_group)
    query_blocks = query_low.astype(jnp.float32)
    key_blocks = key_low.astype(jnp.float32)
    value_blocks = value_low.astype(jnp.float32)
    decay_blocks = log_decay.reshape(head_count, block_count, BLOCK)
    beta_blocks = beta_gate.reshape(head_count, block_count, BLOCK)
    position = jnp.arange(BLOCK)
    lower_mask = position[:, None] >= position[None, :]
    strict_mask = position[:, None] > position[None, :]
    identity_block = jnp.eye(BLOCK, dtype=jnp.float32)
    identity_key = jnp.eye(DK, dtype=jnp.float32)
    cumulative = jnp.cumsum(decay_blocks, axis=-1)
    exponent = jnp.where(lower_mask, cumulative[..., :, None] - cumulative[..., None, :], 0.0)
    damping = jnp.where(lower_mask, jnp.exp(exponent), 0.0)
    key_gram = per_head(
        jnp.einsum("gnik,gnjk->gnij", key_group, key_group, preferred_element_type=jnp.float32)
    )
    system = identity_block + jnp.where(
        strict_mask, beta_blocks[..., :, None] * key_gram * damping, 0.0
    )
    inverse_system = unit_lower_inverse(system, identity_block)
    right_sides = jnp.concatenate(
        [
            beta_blocks[..., None] * value_blocks,
            (beta_blocks * jnp.exp(cumulative))[..., None] * key_blocks,
        ],
        -1,
    )
    solved = block_product(inverse_system, right_sides)
    fresh_values = solved[..., :DV]
    wy_weights = solved[..., DV:]
    scores = (
        per_head(
            jnp.einsum(
                "gnik,gnjk->gnij", query_group, key_group, preferred_element_type=jnp.float32
            )
        )
        * damping
    )
    query_decayed = jnp.exp(cumulative)[..., None] * query_blocks
    last_cum = cumulative[..., -1]
    key_decayed = jnp.exp(last_cum[..., None] - cumulative)[..., None] * key_blocks
    last_gain = jnp.exp(last_cum)
    block_trans = last_gain[..., None, None] * identity_key - jnp.einsum(
        "hnik,hnij->hnkj", key_decayed, wy_weights, precision=exact_matmul_mode
    )
    block_state = jnp.einsum(
        "hnik,hniv->hnkv", key_decayed, fresh_values, precision=exact_matmul_mode
    )

    lanes = lax.axis_size("tp")
    steps = block_count // lanes

    def compose(first, second):
        first_trans, first_state = first
        second_trans, second_state = second
        return (
            block_product(second_trans, first_trans),
            block_product(second_trans, first_state) + second_state,
        )

    level = (block_trans, block_state)
    while level[0].shape[1] > lanes:
        level = compose(
            (level[0][:, 0::2], level[1][:, 0::2]), (level[0][:, 1::2], level[1][:, 1::2])
        )
    lane_trans, lane_state = level
    while level[0].shape[1] > 1:
        level = compose(
            (level[0][:, 0::2], level[1][:, 0::2]), (level[0][:, 1::2], level[1][:, 1::2])
        )
    dev_trans, dev_state = level[0][:, 0], level[1][:, 0]
    zero_state = jnp.zeros((head_count, DK, DV), jnp.float32)

    def relay(turn_index, present_state):
        leaving = matmul_heads(dev_trans, present_state) + dev_state
        return passed_along(leaving.astype(jnp.bfloat16), "ctx", 1).astype(leaving.dtype)

    entering = lax.fori_loop(0, lax.axis_size("ctx") - 1, relay, zero_state)
    lane_entry = [entering]
    for lane in range(1, lanes):
        lane_entry.append(
            matmul_heads(lane_trans[:, lane - 1], lane_entry[-1]) + lane_state[:, lane - 1]
        )
    present_state = jnp.stack(lane_entry, 1)

    def by_step(tensor):
        return tensor.reshape((head_count, lanes, steps) + tensor.shape[2:])

    query_decayed = by_step(query_decayed)
    wy_weights = by_step(wy_weights)
    fresh_values = by_step(fresh_values)
    scores = by_step(scores)
    key_decayed = by_step(key_decayed)
    last_gain = by_step(last_gain)
    gate_values = jax.nn.silu(output_gate.astype(jnp.float32)).reshape(
        lanes, steps, BLOCK, head_count, DV
    )
    tp_index = lax.axis_index("tp")

    def summed_share(partial):
        total = lax.dynamic_index_in_dim(partial, tp_index, 0, keepdims=False).astype(jnp.float32)
        for direction in (1, -1):
            carried = None
            for stage in range(1, lanes):
                target = jnp.clip(tp_index + direction * (lanes - stage), 0, lanes - 1)
                outgoing = lax.dynamic_index_in_dim(partial, target, 0, keepdims=False)
                if carried is not None:
                    outgoing = (outgoing.astype(jnp.float32) + carried.astype(jnp.float32)).astype(
                        jnp.bfloat16
                    )
                if direction == 1:
                    route = [(i, i + 1) for i in range(stage)]
                else:
                    route = [(i, i - 1) for i in range(lanes - stage, lanes)]
                carried = lax.ppermute(outgoing, "tp", route)
            total = total + carried.astype(jnp.float32)
        return total.astype(jnp.bfloat16)

    pieces = []
    for step in range(steps):
        updated_value_rows = fresh_values[:, :, step] - block_product(
            wy_weights[:, :, step], present_state
        )
        emitted = block_product(query_decayed[:, :, step], present_state) + block_product(
            scores[:, :, step], updated_value_rows
        )
        if step + 1 < steps:
            present_state = last_gain[:, :, step][..., None, None] * present_state + jnp.einsum(
                "hnpi,hnpj->hnij",
                key_decayed[:, :, step],
                updated_value_rows,
                precision=exact_matmul_mode,
            )
        attended = emitted.transpose(1, 2, 0, 3)
        scaled = attended * lax.rsqrt(jnp.mean(attended * attended, axis=-1, keepdims=True) + 1e-06)
        normed = (
            (scaled * norm_gain * gate_values[:, step])
            .astype(jnp.bfloat16)
            .reshape(lanes * BLOCK, head_count * DV)
        )
        partial = (
            jnp.dot(normed, out_weight, preferred_element_type=jnp.float32)
            .astype(jnp.bfloat16)
            .reshape(lanes, BLOCK, -1)
        )
        if step + 1 < steps:
            present_state, partial = lax.optimization_barrier((present_state, partial))
        pieces.append(summed_share(partial))
    return jnp.concatenate(pieces, 0)


def solution(mesh):
    in_specs = (
        P("ctx", "tp"),
        P(None, "tp"),
        P("tp", "ctx"),
        P("tp", "ctx"),
        P("ctx", "tp"),
        P(),
        P("tp", None),
    )
    out_specs = P(("ctx", "tp"), None)
    return jax.shard_map(body, mesh=mesh, in_specs=in_specs, out_specs=out_specs, check_vma=False)
```

```python
import jax
import jax.numpy as jnp
from jax import lax
from jax.sharding import PartitionSpec as P

VALUE_HEADS = 32
HK = 16
DK = 128
DV = 128
KCONV = 4
BLOCK = 64


exact_matmul_mode = lax.Precision.HIGH


def passed_along(block, axis, distance):
    devices = range(lax.axis_size(axis))
    route = [(i - distance, i) for i in devices if i - distance in devices]
    return lax.ppermute(block, axis, route)


def l2_rows(tensor):
    return tensor * lax.rsqrt(jnp.sum(tensor * tensor, axis=-1, keepdims=True) + 1e-06)


def matmul_heads(former, latter):
    return jnp.einsum("hij,hjk->hik", former, latter, precision=exact_matmul_mode)


def block_product(former, latter):
    return jnp.einsum("hnij,hnjk->hnik", former, latter, precision=exact_matmul_mode)


def unit_lower_inverse(system, identity_block):
    power = identity_block - system
    inverse = identity_block + power
    for squaring in range(5):
        power = block_product(power, power)
        inverse = inverse + block_product(inverse, power)
    return inverse


def body(qkv_input, conv_weight, log_decay, beta_gate, output_gate, norm_gain, out_weight):
    tokens = qkv_input.shape[0]
    head_ratio = VALUE_HEADS // HK
    group_width = 2 * DK + head_ratio * DV
    group_count = qkv_input.shape[1] // group_width
    head_count = group_count * head_ratio
    block_count = tokens // BLOCK
    last_rows = qkv_input[tokens - (KCONV - 1) :]
    prior_rows = passed_along(last_rows, "ctx", 1)
    padded = jnp.concatenate([prior_rows, qkv_input], 0).astype(jnp.float32)
    conv_taps = conv_weight.astype(jnp.float32)
    mixed = conv_taps[0] * padded[0:tokens]
    for offset in range(1, KCONV):
        mixed = mixed + conv_taps[offset] * padded[offset : offset + tokens]
    activated = jax.nn.silu(mixed)

    def columns(starts, width):
        return jnp.stack([activated[:, start : start + width] for start in starts], 0).reshape(
            len(starts), block_count, BLOCK, width
        )

    group_starts = [group * group_width for group in range(group_count)]
    query_group = (l2_rows(columns(group_starts, DK)) * DK ** (-0.5)).astype(jnp.bfloat16)
    key_group = l2_rows(columns([start + DK for start in group_starts], DK)).astype(jnp.bfloat16)
    value_low = columns(
        [start + 2 * DK + part * DV for start in group_starts for part in range(head_ratio)], DV
    ).astype(jnp.bfloat16)

    def per_head(tensor):
        return jnp.repeat(tensor, head_ratio, axis=0)

    query_low = per_head(query_group)
    key_low = per_head(key_group)
    query_blocks = query_low.astype(jnp.float32)
    key_blocks = key_low.astype(jnp.float32)
    value_blocks = value_low.astype(jnp.float32)
    decay_blocks = log_decay.reshape(head_count, block_count, BLOCK)
    beta_blocks = beta_gate.reshape(head_count, block_count, BLOCK)
    position = jnp.arange(BLOCK)
    lower_mask = position[:, None] >= position[None, :]
    strict_mask = position[:, None] > position[None, :]
    identity_block = jnp.eye(BLOCK, dtype=jnp.float32)
    identity_key = jnp.eye(DK, dtype=jnp.float32)
    cumulative = jnp.cumsum(decay_blocks, axis=-1)
    exponent = jnp.where(lower_mask, cumulative[..., :, None] - cumulative[..., None, :], 0.0)
    damping = jnp.where(lower_mask, jnp.exp(exponent), 0.0)
    key_gram = per_head(
        jnp.einsum("gnik,gnjk->gnij", key_group, key_group, preferred_element_type=jnp.float32)
    )
    system = identity_block + jnp.where(
        strict_mask, beta_blocks[..., :, None] * key_gram * damping, 0.0
    )
    inverse_system = unit_lower_inverse(system, identity_block)
    right_sides = jnp.concatenate(
        [
            beta_blocks[..., None] * value_blocks,
            (beta_blocks * jnp.exp(cumulative))[..., None] * key_blocks,
        ],
        -1,
    )
    solved = block_product(inverse_system, right_sides)
    fresh_values = solved[..., :DV]
    wy_weights = solved[..., DV:]
    scores = (
        per_head(
            jnp.einsum(
                "gnik,gnjk->gnij", query_group, key_group, preferred_element_type=jnp.float32
            )
        )
        * damping
    )
    query_decayed = jnp.exp(cumulative)[..., None] * query_blocks
    last_cum = cumulative[..., -1]
    key_decayed = jnp.exp(last_cum[..., None] - cumulative)[..., None] * key_blocks
    last_gain = jnp.exp(last_cum)
    block_trans = last_gain[..., None, None] * identity_key - jnp.einsum(
        "hnik,hnij->hnkj", key_decayed, wy_weights, precision=exact_matmul_mode
    )
    block_state = jnp.einsum(
        "hnik,hniv->hnkv", key_decayed, fresh_values, precision=exact_matmul_mode
    )

    lanes = lax.axis_size("tp")
    steps = block_count // lanes

    def compose(first, second):
        first_trans, first_state = first
        second_trans, second_state = second
        return (
            block_product(second_trans, first_trans),
            block_product(second_trans, first_state) + second_state,
        )

    level = (block_trans, block_state)
    while level[0].shape[1] > lanes:
        level = compose(
            (level[0][:, 0::2], level[1][:, 0::2]), (level[0][:, 1::2], level[1][:, 1::2])
        )
    lane_trans, lane_state = level
    while level[0].shape[1] > 1:
        level = compose(
            (level[0][:, 0::2], level[1][:, 0::2]), (level[0][:, 1::2], level[1][:, 1::2])
        )
    dev_trans, dev_state = level[0][:, 0], level[1][:, 0]
    zero_state = jnp.zeros((head_count, DK, DV), jnp.float32)

    def relay(turn_index, present_state):
        leaving = matmul_heads(dev_trans, present_state) + dev_state
        return passed_along(leaving.astype(jnp.bfloat16), "ctx", 1).astype(leaving.dtype)

    entering = lax.fori_loop(0, lax.axis_size("ctx") - 1, relay, zero_state)
    lane_entry = [entering]
    for lane in range(1, lanes):
        lane_entry.append(
            matmul_heads(lane_trans[:, lane - 1], lane_entry[-1]) + lane_state[:, lane - 1]
        )
    present_state = jnp.stack(lane_entry, 1)

    def by_step(tensor):
        return tensor.reshape((head_count, lanes, steps) + tensor.shape[2:])

    query_decayed = by_step(query_decayed)
    wy_weights = by_step(wy_weights)
    fresh_values = by_step(fresh_values)
    scores = by_step(scores)
    key_decayed = by_step(key_decayed)
    last_gain = by_step(last_gain)
    gate_values = jax.nn.silu(output_gate.astype(jnp.float32)).reshape(
        lanes, steps, BLOCK, head_count, DV
    )
    tp_index = lax.axis_index("tp")

    def summed_share(partial):
        total = lax.dynamic_index_in_dim(partial, tp_index, 0, keepdims=False).astype(jnp.float32)
        for direction in (1, -1):
            carried = None
            for stage in range(1, lanes):
                target = jnp.clip(tp_index + direction * (lanes - stage), 0, lanes - 1)
                outgoing = lax.dynamic_index_in_dim(partial, target, 0, keepdims=False)
                if carried is not None:
                    outgoing = (outgoing.astype(jnp.float32) + carried.astype(jnp.float32)).astype(
                        jnp.bfloat16
                    )
                if direction == 1:
                    route = [(i, i + 1) for i in range(stage)]
                else:
                    route = [(i, i - 1) for i in range(lanes - stage, lanes)]
                carried = lax.ppermute(outgoing, "tp", route)
            total = total + carried.astype(jnp.float32)
        return total.astype(jnp.bfloat16)

    pieces = []
    for step in range(steps):
        updated_value_rows = fresh_values[:, :, step] - block_product(
            wy_weights[:, :, step], present_state
        )
        emitted = block_product(query_decayed[:, :, step], present_state) + block_product(
            scores[:, :, step], updated_value_rows
        )
        if step + 1 < steps:
            present_state = last_gain[:, :, step][..., None, None] * present_state + jnp.einsum(
                "hnpi,hnpj->hnij",
                key_decayed[:, :, step],
                updated_value_rows,
                precision=exact_matmul_mode,
            )
        attended = emitted.transpose(1, 2, 0, 3)
        scaled = attended * lax.rsqrt(jnp.mean(attended * attended, axis=-1, keepdims=True) + 1e-06)
        normed = (
            (scaled * norm_gain * gate_values[:, step])
            .astype(jnp.bfloat16)
            .reshape(lanes * BLOCK, head_count * DV)
        )
        partial = (
            jnp.dot(normed, out_weight, preferred_element_type=jnp.float32)
            .astype(jnp.bfloat16)
            .reshape(lanes, BLOCK, -1)
        )
        pieces.append(partial)
    return summed_share(jnp.stack(pieces, 1).reshape(lanes, steps * BLOCK, -1))


def solution(mesh):
    in_specs = (
        P("ctx", "tp"),
        P(None, "tp"),
        P("tp", "ctx"),
        P("tp", "ctx"),
        P("ctx", "tp"),
        P(),
        P("tp", None),
    )
    out_specs = P(("ctx", "tp"), None)
    return jax.shard_map(body, mesh=mesh, in_specs=in_specs, out_specs=out_specs, check_vma=False)
```

```python
import jax
import jax.numpy as jnp
from jax import lax
from jax.sharding import PartitionSpec as P

VALUE_HEADS = 32
HK = 16
DK = 128
DV = 128
KCONV = 4
BLOCK = 64


exact_matmul_mode = lax.Precision.HIGH


def passed_along(block, axis, distance):
    devices = range(lax.axis_size(axis))
    route = [(i - distance, i) for i in devices if i - distance in devices]
    return lax.ppermute(block, axis, route)


def l2_rows(tensor):
    return tensor * lax.rsqrt(jnp.sum(tensor * tensor, axis=-1, keepdims=True) + 1e-06)


def matmul_heads(former, latter):
    return jnp.einsum("hij,hjk->hik", former, latter, precision=exact_matmul_mode)


def block_product(former, latter):
    return jnp.einsum("hnij,hnjk->hnik", former, latter, precision=exact_matmul_mode)


def unit_lower_inverse(system, identity_block):
    power = identity_block - system
    inverse = identity_block + power
    for squaring in range(5):
        power = block_product(power, power)
        inverse = inverse + block_product(inverse, power)
    return inverse


def body(qkv_input, conv_weight, log_decay, beta_gate, output_gate, norm_gain, out_weight):
    tokens = qkv_input.shape[0]
    head_ratio = VALUE_HEADS // HK
    group_width = 2 * DK + head_ratio * DV
    group_count = qkv_input.shape[1] // group_width
    head_count = group_count * head_ratio
    block_count = tokens // BLOCK
    last_rows = qkv_input[tokens - (KCONV - 1) :]
    prior_rows = passed_along(last_rows, "ctx", 1)
    padded = jnp.concatenate([prior_rows, qkv_input], 0).astype(jnp.float32)
    conv_taps = conv_weight.astype(jnp.float32)
    mixed = conv_taps[0] * padded[0:tokens]
    for offset in range(1, KCONV):
        mixed = mixed + conv_taps[offset] * padded[offset : offset + tokens]
    activated = jax.nn.silu(mixed)

    def columns(starts, width):
        return jnp.stack([activated[:, start : start + width] for start in starts], 0).reshape(
            len(starts), block_count, BLOCK, width
        )

    group_starts = [group * group_width for group in range(group_count)]
    query_group = (l2_rows(columns(group_starts, DK)) * DK ** (-0.5)).astype(jnp.bfloat16)
    key_group = l2_rows(columns([start + DK for start in group_starts], DK)).astype(jnp.bfloat16)
    value_low = columns(
        [start + 2 * DK + part * DV for start in group_starts for part in range(head_ratio)], DV
    ).astype(jnp.bfloat16)

    def per_head(tensor):
        return jnp.repeat(tensor, head_ratio, axis=0)

    query_low = per_head(query_group)
    key_low = per_head(key_group)
    query_blocks = query_low.astype(jnp.float32)
    key_blocks = key_low.astype(jnp.float32)
    value_blocks = value_low.astype(jnp.float32)
    decay_blocks = log_decay.reshape(head_count, block_count, BLOCK)
    beta_blocks = beta_gate.reshape(head_count, block_count, BLOCK)
    position = jnp.arange(BLOCK)
    lower_mask = position[:, None] >= position[None, :]
    strict_mask = position[:, None] > position[None, :]
    identity_block = jnp.eye(BLOCK, dtype=jnp.float32)
    identity_key = jnp.eye(DK, dtype=jnp.float32)
    cumulative = jnp.cumsum(decay_blocks, axis=-1)
    exponent = jnp.where(lower_mask, cumulative[..., :, None] - cumulative[..., None, :], 0.0)
    damping = jnp.where(lower_mask, jnp.exp(exponent), 0.0)
    key_gram = per_head(
        jnp.einsum("gnik,gnjk->gnij", key_group, key_group, preferred_element_type=jnp.float32)
    )
    system = identity_block + jnp.where(
        strict_mask, beta_blocks[..., :, None] * key_gram * damping, 0.0
    )
    inverse_system = unit_lower_inverse(system, identity_block)
    right_sides = jnp.concatenate(
        [
            beta_blocks[..., None] * value_blocks,
            (beta_blocks * jnp.exp(cumulative))[..., None] * key_blocks,
        ],
        -1,
    )
    solved = block_product(inverse_system, right_sides)
    fresh_values = solved[..., :DV]
    wy_weights = solved[..., DV:]
    scores = (
        per_head(
            jnp.einsum(
                "gnik,gnjk->gnij", query_group, key_group, preferred_element_type=jnp.float32
            )
        )
        * damping
    )
    query_decayed = jnp.exp(cumulative)[..., None] * query_blocks
    last_cum = cumulative[..., -1]
    key_decayed = jnp.exp(last_cum[..., None] - cumulative)[..., None] * key_blocks
    last_gain = jnp.exp(last_cum)
    block_trans = last_gain[..., None, None] * identity_key - jnp.einsum(
        "hnik,hnij->hnkj", key_decayed, wy_weights, precision=exact_matmul_mode
    )
    block_state = jnp.einsum(
        "hnik,hniv->hnkv", key_decayed, fresh_values, precision=exact_matmul_mode
    )

    lanes = lax.axis_size("tp")
    steps = block_count // lanes

    def compose(first, second):
        first_trans, first_state = first
        second_trans, second_state = second
        return (
            block_product(second_trans, first_trans),
            block_product(second_trans, first_state) + second_state,
        )

    level = (block_trans, block_state)
    while level[0].shape[1] > lanes:
        level = compose(
            (level[0][:, 0::2], level[1][:, 0::2]), (level[0][:, 1::2], level[1][:, 1::2])
        )
    lane_trans, lane_state = level
    while level[0].shape[1] > 1:
        level = compose(
            (level[0][:, 0::2], level[1][:, 0::2]), (level[0][:, 1::2], level[1][:, 1::2])
        )
    dev_trans, dev_state = level[0][:, 0], level[1][:, 0]
    zero_state = jnp.zeros((head_count, DK, DV), jnp.float32)

    def relay(turn_index, present_state):
        leaving = matmul_heads(dev_trans, present_state) + dev_state
        return passed_along(leaving.astype(jnp.bfloat16), "ctx", 1).astype(leaving.dtype)

    entering = lax.fori_loop(0, lax.axis_size("ctx") - 1, relay, zero_state)
    lane_entry = [entering]
    for lane in range(1, lanes):
        lane_entry.append(
            matmul_heads(lane_trans[:, lane - 1], lane_entry[-1]) + lane_state[:, lane - 1]
        )
    present_state = jnp.stack(lane_entry, 1)

    def by_step(tensor):
        return tensor.reshape((head_count, lanes, steps) + tensor.shape[2:])

    query_decayed = by_step(query_decayed)
    wy_weights = by_step(wy_weights)
    fresh_values = by_step(fresh_values)
    scores = by_step(scores)
    key_decayed = by_step(key_decayed)
    last_gain = by_step(last_gain)
    gate_values = jax.nn.silu(output_gate.astype(jnp.float32)).reshape(
        lanes, steps, BLOCK, head_count, DV
    )
    tp_index = lax.axis_index("tp")

    def exchange_stage(share):
        stage = share["stage"] + 1
        for direction in (1, -1):
            target = jnp.clip(tp_index + direction * (lanes - stage), 0, lanes - 1)
            outgoing = lax.dynamic_index_in_dim(share["partial"], target, 0, keepdims=False)
            if stage > 1:
                outgoing = (
                    outgoing.astype(jnp.float32) + share[direction].astype(jnp.float32)
                ).astype(jnp.bfloat16)
            if direction == 1:
                route = [(i, i + 1) for i in range(stage)]
            else:
                route = [(i, i - 1) for i in range(lanes - stage, lanes)]
            share[direction] = lax.ppermute(outgoing, "tp", route)
        share["stage"] = stage

    def share_total(share):
        total = lax.dynamic_index_in_dim(share["partial"], tp_index, 0, keepdims=False)
        total = total.astype(jnp.float32) + share[1].astype(jnp.float32)
        return (total + share[-1].astype(jnp.float32)).astype(jnp.bfloat16)

    shares = []
    for step in range(steps):
        updated_value_rows = fresh_values[:, :, step] - block_product(
            wy_weights[:, :, step], present_state
        )
        emitted = block_product(query_decayed[:, :, step], present_state) + block_product(
            scores[:, :, step], updated_value_rows
        )
        if step + 1 < steps:
            present_state = last_gain[:, :, step][..., None, None] * present_state + jnp.einsum(
                "hnpi,hnpj->hnij",
                key_decayed[:, :, step],
                updated_value_rows,
                precision=exact_matmul_mode,
            )
        attended = emitted.transpose(1, 2, 0, 3)
        scaled = attended * lax.rsqrt(jnp.mean(attended * attended, axis=-1, keepdims=True) + 1e-06)
        normed = (
            (scaled * norm_gain * gate_values[:, step])
            .astype(jnp.bfloat16)
            .reshape(lanes * BLOCK, head_count * DV)
        )
        partial = (
            jnp.dot(normed, out_weight, preferred_element_type=jnp.float32)
            .astype(jnp.bfloat16)
            .reshape(lanes, BLOCK, -1)
        )
        open_shares = [share for share in shares if share["stage"] < lanes - 1]
        if step + 1 < steps:
            landed = [(share[1], share[-1]) for share in open_shares]
            present_state, partial, landed = lax.optimization_barrier(
                (present_state, partial, landed)
            )
            for share, (right, left) in zip(open_shares, landed):
                share[1], share[-1] = right, left
        shares.append({"partial": partial, "stage": 0})
        for share in shares:
            if share["stage"] < lanes - 1:
                exchange_stage(share)
    while any(share["stage"] < lanes - 1 for share in shares):
        for share in shares:
            if share["stage"] < lanes - 1:
                exchange_stage(share)
    return jnp.concatenate([share_total(share) for share in shares], 0)


def solution(mesh):
    in_specs = (
        P("ctx", "tp"),
        P(None, "tp"),
        P("tp", "ctx"),
        P("tp", "ctx"),
        P("ctx", "tp"),
        P(),
        P("tp", None),
    )
    out_specs = P(("ctx", "tp"), None)
    return jax.shard_map(body, mesh=mesh, in_specs=in_specs, out_specs=out_specs, check_vma=False)
```

```python
import jax
import jax.numpy as jnp
from jax import lax
from jax.sharding import PartitionSpec as P

VALUE_HEADS = 32
HK = 16
DK = 128
DV = 128
KCONV = 4
BLOCK = 64


exact_matmul_mode = lax.Precision.HIGH


def passed_along(block, axis, distance):
    devices = range(lax.axis_size(axis))
    route = [(i - distance, i) for i in devices if i - distance in devices]
    return lax.ppermute(block, axis, route)


def l2_rows(tensor):
    return tensor * lax.rsqrt(jnp.sum(tensor * tensor, axis=-1, keepdims=True) + 1e-06)


def matmul_heads(former, latter):
    return jnp.einsum("hij,hjk->hik", former, latter, precision=exact_matmul_mode)


def block_product(former, latter):
    return jnp.einsum("hnij,hnjk->hnik", former, latter, precision=exact_matmul_mode)


def unit_lower_inverse(system, identity_block):
    power = identity_block - system
    inverse = identity_block + power
    for squaring in range(5):
        power = block_product(power, power)
        inverse = inverse + block_product(inverse, power)
    return inverse


def body(qkv_input, conv_weight, log_decay, beta_gate, output_gate, norm_gain, out_weight):
    tokens = qkv_input.shape[0]
    head_ratio = VALUE_HEADS // HK
    group_width = 2 * DK + head_ratio * DV
    group_count = qkv_input.shape[1] // group_width
    head_count = group_count * head_ratio
    block_count = tokens // BLOCK
    last_rows = qkv_input[tokens - (KCONV - 1) :]
    prior_rows = passed_along(last_rows, "ctx", 1)
    padded = jnp.concatenate([prior_rows, qkv_input], 0).astype(jnp.float32)
    conv_taps = conv_weight.astype(jnp.float32)
    mixed = conv_taps[0] * padded[0:tokens]
    for offset in range(1, KCONV):
        mixed = mixed + conv_taps[offset] * padded[offset : offset + tokens]
    activated = jax.nn.silu(mixed)

    def columns(starts, width):
        return jnp.stack([activated[:, start : start + width] for start in starts], 0).reshape(
            len(starts), block_count, BLOCK, width
        )

    group_starts = [group * group_width for group in range(group_count)]
    query_group = (l2_rows(columns(group_starts, DK)) * DK ** (-0.5)).astype(jnp.bfloat16)
    key_group = l2_rows(columns([start + DK for start in group_starts], DK)).astype(jnp.bfloat16)
    value_low = columns(
        [start + 2 * DK + part * DV for start in group_starts for part in range(head_ratio)], DV
    ).astype(jnp.bfloat16)

    def per_head(tensor):
        return jnp.repeat(tensor, head_ratio, axis=0)

    query_low = per_head(query_group)
    key_low = per_head(key_group)
    query_blocks = query_low.astype(jnp.float32)
    key_blocks = key_low.astype(jnp.float32)
    value_blocks = value_low.astype(jnp.float32)
    decay_blocks = log_decay.reshape(head_count, block_count, BLOCK)
    beta_blocks = beta_gate.reshape(head_count, block_count, BLOCK)
    position = jnp.arange(BLOCK)
    lower_mask = position[:, None] >= position[None, :]
    strict_mask = position[:, None] > position[None, :]
    identity_block = jnp.eye(BLOCK, dtype=jnp.float32)
    identity_key = jnp.eye(DK, dtype=jnp.float32)
    cumulative = jnp.cumsum(decay_blocks, axis=-1)
    exponent = jnp.where(lower_mask, cumulative[..., :, None] - cumulative[..., None, :], 0.0)
    damping = jnp.where(lower_mask, jnp.exp(exponent), 0.0)
    key_gram = per_head(
        jnp.einsum("gnik,gnjk->gnij", key_group, key_group, preferred_element_type=jnp.float32)
    )
    system = identity_block + jnp.where(
        strict_mask, beta_blocks[..., :, None] * key_gram * damping, 0.0
    )
    inverse_system = unit_lower_inverse(system, identity_block)
    right_sides = jnp.concatenate(
        [
            beta_blocks[..., None] * value_blocks,
            (beta_blocks * jnp.exp(cumulative))[..., None] * key_blocks,
        ],
        -1,
    )
    solved = block_product(inverse_system, right_sides)
    fresh_values = solved[..., :DV]
    wy_weights = solved[..., DV:]
    scores = (
        per_head(
            jnp.einsum(
                "gnik,gnjk->gnij", query_group, key_group, preferred_element_type=jnp.float32
            )
        )
        * damping
    )
    query_decayed = jnp.exp(cumulative)[..., None] * query_blocks
    last_cum = cumulative[..., -1]
    key_decayed = jnp.exp(last_cum[..., None] - cumulative)[..., None] * key_blocks
    last_gain = jnp.exp(last_cum)
    block_trans = last_gain[..., None, None] * identity_key - jnp.einsum(
        "hnik,hnij->hnkj", key_decayed, wy_weights, precision=exact_matmul_mode
    )
    block_state = jnp.einsum(
        "hnik,hniv->hnkv", key_decayed, fresh_values, precision=exact_matmul_mode
    )

    lanes = lax.axis_size("tp")
    steps = block_count // lanes

    def compose(first, second):
        first_trans, first_state = first
        second_trans, second_state = second
        return (
            block_product(second_trans, first_trans),
            block_product(second_trans, first_state) + second_state,
        )

    level = (block_trans, block_state)
    while level[0].shape[1] > lanes:
        level = compose(
            (level[0][:, 0::2], level[1][:, 0::2]), (level[0][:, 1::2], level[1][:, 1::2])
        )
    lane_trans, lane_state = level
    while level[0].shape[1] > 1:
        level = compose(
            (level[0][:, 0::2], level[1][:, 0::2]), (level[0][:, 1::2], level[1][:, 1::2])
        )
    dev_trans, dev_state = level[0][:, 0], level[1][:, 0]
    zero_state = jnp.zeros((head_count, DK, DV), jnp.float32)

    acc_trans, acc_state = dev_trans, dev_state
    distance = 1
    while distance < lax.axis_size("ctx"):
        if 2 * distance < lax.axis_size("ctx"):
            earlier = passed_along(
                jnp.concatenate([acc_trans, acc_state], -1).astype(jnp.bfloat16), "ctx", distance
            ).astype(jnp.float32)
            composed = matmul_heads(acc_trans, earlier)
            acc_trans, acc_state = composed[..., :DK], composed[..., DK:] + acc_state
        else:
            earlier = passed_along(acc_state.astype(jnp.bfloat16), "ctx", distance)
            acc_state = matmul_heads(acc_trans, earlier.astype(jnp.float32)) + acc_state
        distance *= 2
    entering = passed_along(acc_state.astype(jnp.bfloat16), "ctx", 1).astype(jnp.float32)
    lane_entry = [entering]
    for lane in range(1, lanes):
        lane_entry.append(
            matmul_heads(lane_trans[:, lane - 1], lane_entry[-1]) + lane_state[:, lane - 1]
        )
    present_state = jnp.stack(lane_entry, 1)

    def by_step(tensor):
        return tensor.reshape((head_count, lanes, steps) + tensor.shape[2:])

    query_decayed = by_step(query_decayed)
    wy_weights = by_step(wy_weights)
    fresh_values = by_step(fresh_values)
    scores = by_step(scores)
    key_decayed = by_step(key_decayed)
    last_gain = by_step(last_gain)
    gate_values = jax.nn.silu(output_gate.astype(jnp.float32)).reshape(
        lanes, steps, BLOCK, head_count, DV
    )
    tp_index = lax.axis_index("tp")

    def summed_share(partial):
        total = lax.dynamic_index_in_dim(partial, tp_index, 0, keepdims=False).astype(jnp.float32)
        for direction in (1, -1):
            carried = None
            for stage in range(1, lanes):
                target = jnp.clip(tp_index + direction * (lanes - stage), 0, lanes - 1)
                outgoing = lax.dynamic_index_in_dim(partial, target, 0, keepdims=False)
                if carried is not None:
                    outgoing = (outgoing.astype(jnp.float32) + carried.astype(jnp.float32)).astype(
                        jnp.bfloat16
                    )
                if direction == 1:
                    route = [(i, i + 1) for i in range(stage)]
                else:
                    route = [(i, i - 1) for i in range(lanes - stage, lanes)]
                carried = lax.ppermute(outgoing, "tp", route)
            total = total + carried.astype(jnp.float32)
        return total.astype(jnp.bfloat16)

    pieces = []
    for step in range(steps):
        updated_value_rows = fresh_values[:, :, step] - block_product(
            wy_weights[:, :, step], present_state
        )
        emitted = block_product(query_decayed[:, :, step], present_state) + block_product(
            scores[:, :, step], updated_value_rows
        )
        if step + 1 < steps:
            present_state = last_gain[:, :, step][..., None, None] * present_state + jnp.einsum(
                "hnpi,hnpj->hnij",
                key_decayed[:, :, step],
                updated_value_rows,
                precision=exact_matmul_mode,
            )
        attended = emitted.transpose(1, 2, 0, 3)
        scaled = attended * lax.rsqrt(jnp.mean(attended * attended, axis=-1, keepdims=True) + 1e-06)
        normed = (
            (scaled * norm_gain * gate_values[:, step])
            .astype(jnp.bfloat16)
            .reshape(lanes * BLOCK, head_count * DV)
        )
        partial = (
            jnp.dot(normed, out_weight, preferred_element_type=jnp.float32)
            .astype(jnp.bfloat16)
            .reshape(lanes, BLOCK, -1)
        )
        if step + 1 < steps:
            present_state, partial = lax.optimization_barrier((present_state, partial))
        pieces.append(summed_share(partial))
    return jnp.concatenate(pieces, 0)


def solution(mesh):
    in_specs = (
        P("ctx", "tp"),
        P(None, "tp"),
        P("tp", "ctx"),
        P("tp", "ctx"),
        P("ctx", "tp"),
        P(),
        P("tp", None),
    )
    out_specs = P(("ctx", "tp"), None)
    return jax.shard_map(body, mesh=mesh, in_specs=in_specs, out_specs=out_specs, check_vma=False)
```

```python
import jax
import jax.numpy as jnp
from jax import lax
from jax.sharding import PartitionSpec as P

VALUE_HEADS = 32
HK = 16
DK = 128
DV = 128
KCONV = 4
BLOCK = 64


exact_matmul_mode = lax.Precision.HIGH


def passed_along(block, axis, distance):
    devices = range(lax.axis_size(axis))
    route = [(i - distance, i) for i in devices if i - distance in devices]
    return lax.ppermute(block, axis, route)


def l2_rows(tensor):
    return tensor * lax.rsqrt(jnp.sum(tensor * tensor, axis=-1, keepdims=True) + 1e-06)


def matmul_heads(former, latter):
    return jnp.einsum("hij,hjk->hik", former, latter, precision=exact_matmul_mode)


def block_product(former, latter):
    return jnp.einsum("hnij,hnjk->hnik", former, latter, precision=exact_matmul_mode)


def unit_lower_inverse(system, identity_block):
    power = identity_block - system
    inverse = identity_block + power
    for squaring in range(5):
        power = block_product(power, power)
        inverse = inverse + block_product(inverse, power)
    return inverse


def body(qkv_input, conv_weight, log_decay, beta_gate, output_gate, norm_gain, out_weight):
    tokens = qkv_input.shape[0]
    head_ratio = VALUE_HEADS // HK
    group_width = 2 * DK + head_ratio * DV
    group_count = qkv_input.shape[1] // group_width
    head_count = group_count * head_ratio
    block_count = tokens // BLOCK
    last_rows = qkv_input[tokens - (KCONV - 1) :]
    prior_rows = passed_along(last_rows, "ctx", 1)
    padded = jnp.concatenate([prior_rows, qkv_input], 0).astype(jnp.float32)
    conv_taps = conv_weight.astype(jnp.float32)
    mixed = conv_taps[0] * padded[0:tokens]
    for offset in range(1, KCONV):
        mixed = mixed + conv_taps[offset] * padded[offset : offset + tokens]
    activated = jax.nn.silu(mixed)

    def columns(starts, width):
        return jnp.stack([activated[:, start : start + width] for start in starts], 0).reshape(
            len(starts), block_count, BLOCK, width
        )

    group_starts = [group * group_width for group in range(group_count)]
    query_group = (l2_rows(columns(group_starts, DK)) * DK ** (-0.5)).astype(jnp.bfloat16)
    key_group = l2_rows(columns([start + DK for start in group_starts], DK)).astype(jnp.bfloat16)
    value_low = columns(
        [start + 2 * DK + part * DV for start in group_starts for part in range(head_ratio)], DV
    ).astype(jnp.bfloat16)

    def per_head(tensor):
        return jnp.repeat(tensor, head_ratio, axis=0)

    query_low = per_head(query_group)
    key_low = per_head(key_group)
    query_blocks = query_low.astype(jnp.float32)
    key_blocks = key_low.astype(jnp.float32)
    value_blocks = value_low.astype(jnp.float32)
    decay_blocks = log_decay.reshape(head_count, block_count, BLOCK)
    beta_blocks = beta_gate.reshape(head_count, block_count, BLOCK)
    position = jnp.arange(BLOCK)
    lower_mask = position[:, None] >= position[None, :]
    strict_mask = position[:, None] > position[None, :]
    identity_block = jnp.eye(BLOCK, dtype=jnp.float32)
    identity_key = jnp.eye(DK, dtype=jnp.float32)
    cumulative = jnp.cumsum(decay_blocks, axis=-1)
    exponent = jnp.where(lower_mask, cumulative[..., :, None] - cumulative[..., None, :], 0.0)
    damping = jnp.where(lower_mask, jnp.exp(exponent), 0.0)
    key_gram = per_head(
        jnp.einsum("gnik,gnjk->gnij", key_group, key_group, preferred_element_type=jnp.float32)
    )
    system = identity_block + jnp.where(
        strict_mask, beta_blocks[..., :, None] * key_gram * damping, 0.0
    )
    inverse_system = unit_lower_inverse(system, identity_block)
    right_sides = jnp.concatenate(
        [
            beta_blocks[..., None] * value_blocks,
            (beta_blocks * jnp.exp(cumulative))[..., None] * key_blocks,
        ],
        -1,
    )
    solved = block_product(inverse_system, right_sides)
    fresh_values = solved[..., :DV]
    wy_weights = solved[..., DV:]
    scores = (
        per_head(
            jnp.einsum(
                "gnik,gnjk->gnij", query_group, key_group, preferred_element_type=jnp.float32
            )
        )
        * damping
    )
    query_decayed = jnp.exp(cumulative)[..., None] * query_blocks
    last_cum = cumulative[..., -1]
    key_decayed = jnp.exp(last_cum[..., None] - cumulative)[..., None] * key_blocks
    last_gain = jnp.exp(last_cum)
    key_solved = jnp.einsum(
        "hnik,hnij->hnkj", key_decayed, solved, precision=exact_matmul_mode
    )
    block_level = jnp.concatenate(
        [last_gain[..., None, None] * identity_key - key_solved[..., DV:], key_solved[..., :DV]], -1
    )

    lanes = lax.axis_size("tp")
    steps = block_count // lanes

    def compose_level(level):
        pairs = level.reshape((head_count, level.shape[1] // 2, 2) + level.shape[2:])
        first, second = pairs[:, :, 0], pairs[:, :, 1]
        carried_state = jnp.concatenate([jnp.zeros_like(second[..., :DK]), second[..., DK:]], -1)
        return block_product(second[..., :DK], first) + carried_state

    level = block_level
    while level.shape[1] > lanes:
        level = compose_level(level)
    lane_trans, lane_state = level[..., :DK], level[..., DK:]
    while level.shape[1] > 1:
        level = compose_level(level)
    dev_trans, dev_state = level[:, 0, :, :DK], level[:, 0, :, DK:]
    zero_state = jnp.zeros((head_count, DK, DV), jnp.float32)

    acc_trans, acc_state = dev_trans, dev_state
    distance = 1
    while distance < lax.axis_size("ctx"):
        if 2 * distance < lax.axis_size("ctx"):
            earlier = passed_along(
                jnp.concatenate([acc_trans, acc_state], -1).astype(jnp.bfloat16), "ctx", distance
            ).astype(jnp.float32)
            composed = matmul_heads(acc_trans, earlier)
            acc_trans, acc_state = composed[..., :DK], composed[..., DK:] + acc_state
        else:
            earlier = passed_along(acc_state.astype(jnp.bfloat16), "ctx", distance)
            acc_state = matmul_heads(acc_trans, earlier.astype(jnp.float32)) + acc_state
        distance *= 2
    entering = passed_along(acc_state.astype(jnp.bfloat16), "ctx", 1).astype(jnp.float32)
    lane_entry = [entering]
    for lane in range(1, lanes):
        lane_entry.append(
            matmul_heads(lane_trans[:, lane - 1], lane_entry[-1]) + lane_state[:, lane - 1]
        )
    present_state = jnp.stack(lane_entry, 1)

    def by_step(tensor):
        return tensor.reshape((head_count, lanes, steps) + tensor.shape[2:])

    query_decayed = by_step(query_decayed)
    wy_weights = by_step(wy_weights)
    fresh_values = by_step(fresh_values)
    scores = by_step(scores)
    key_decayed = by_step(key_decayed)
    last_gain = by_step(last_gain)
    gate_values = jax.nn.silu(output_gate.astype(jnp.float32)).reshape(
        lanes, steps, BLOCK, head_count, DV
    )
    tp_index = lax.axis_index("tp")

    def summed_share(partial):
        total = lax.dynamic_index_in_dim(partial, tp_index, 0, keepdims=False).astype(jnp.float32)
        for direction in (1, -1):
            carried = None
            for stage in range(1, lanes):
                target = jnp.clip(tp_index + direction * (lanes - stage), 0, lanes - 1)
                outgoing = lax.dynamic_index_in_dim(partial, target, 0, keepdims=False)
                if carried is not None:
                    outgoing = (outgoing.astype(jnp.float32) + carried.astype(jnp.float32)).astype(
                        jnp.bfloat16
                    )
                if direction == 1:
                    route = [(i, i + 1) for i in range(stage)]
                else:
                    route = [(i, i - 1) for i in range(lanes - stage, lanes)]
                carried = lax.ppermute(outgoing, "tp", route)
            total = total + carried.astype(jnp.float32)
        return total.astype(jnp.bfloat16)

    pieces = []
    for step in range(steps):
        updated_value_rows = fresh_values[:, :, step] - block_product(
            wy_weights[:, :, step], present_state
        )
        emitted = block_product(query_decayed[:, :, step], present_state) + block_product(
            scores[:, :, step], updated_value_rows
        )
        if step + 1 < steps:
            present_state = last_gain[:, :, step][..., None, None] * present_state + jnp.einsum(
                "hnpi,hnpj->hnij",
                key_decayed[:, :, step],
                updated_value_rows,
                precision=exact_matmul_mode,
            )
        attended = emitted.transpose(1, 2, 0, 3)
        scaled = attended * lax.rsqrt(jnp.mean(attended * attended, axis=-1, keepdims=True) + 1e-06)
        normed = (
            (scaled * norm_gain * gate_values[:, step])
            .astype(jnp.bfloat16)
            .reshape(lanes * BLOCK, head_count * DV)
        )
        partial = (
            jnp.dot(normed, out_weight, preferred_element_type=jnp.float32)
            .astype(jnp.bfloat16)
            .reshape(lanes, BLOCK, -1)
        )
        if step + 1 < steps:
            present_state, partial = lax.optimization_barrier((present_state, partial))
        pieces.append(summed_share(partial))
    return jnp.concatenate(pieces, 0)


def solution(mesh):
    in_specs = (
        P("ctx", "tp"),
        P(None, "tp"),
        P("tp", "ctx"),
        P("tp", "ctx"),
        P("ctx", "tp"),
        P(),
        P("tp", None),
    )
    out_specs = P(("ctx", "tp"), None)
    return jax.shard_map(body, mesh=mesh, in_specs=in_specs, out_specs=out_specs, check_vma=False)
```

```python
import jax
import jax.numpy as jnp
from jax import lax
from jax.sharding import PartitionSpec as P

VALUE_HEADS = 32
HK = 16
DK = 128
DV = 128
KCONV = 4
BLOCK = 64


exact_matmul_mode = lax.Precision.HIGH


def passed_along(block, axis, distance):
    devices = range(lax.axis_size(axis))
    route = [(i - distance, i) for i in devices if i - distance in devices]
    return lax.ppermute(block, axis, route)


def l2_rows(tensor):
    return tensor * lax.rsqrt(jnp.sum(tensor * tensor, axis=-1, keepdims=True) + 1e-06)


def matmul_heads(former, latter):
    return jnp.einsum("hij,hjk->hik", former, latter, precision=exact_matmul_mode)


def block_product(former, latter):
    return jnp.einsum("hnij,hnjk->hnik", former, latter, precision=exact_matmul_mode)


def unit_lower_inverse(system, identity_block):
    power = identity_block - system
    inverse = identity_block + power
    for squaring in range(5):
        power = block_product(power, power)
        inverse = inverse + block_product(inverse, power)
    return inverse


def body(qkv_input, conv_weight, log_decay, beta_gate, output_gate, norm_gain, out_weight):
    tokens = qkv_input.shape[0]
    head_ratio = VALUE_HEADS // HK
    group_width = 2 * DK + head_ratio * DV
    group_count = qkv_input.shape[1] // group_width
    head_count = group_count * head_ratio
    block_count = tokens // BLOCK
    last_rows = qkv_input[tokens - (KCONV - 1) :]
    prior_rows = passed_along(last_rows, "ctx", 1)
    padded = jnp.concatenate([prior_rows, qkv_input], 0).astype(jnp.float32)
    conv_taps = conv_weight.astype(jnp.float32)
    mixed = conv_taps[0] * padded[0:tokens]
    for offset in range(1, KCONV):
        mixed = mixed + conv_taps[offset] * padded[offset : offset + tokens]
    activated = jax.nn.silu(mixed)

    def columns(starts, width):
        return jnp.stack([activated[:, start : start + width] for start in starts], 0).reshape(
            len(starts), block_count, BLOCK, width
        )

    group_starts = [group * group_width for group in range(group_count)]
    query_group = (l2_rows(columns(group_starts, DK)) * DK ** (-0.5)).astype(jnp.bfloat16)
    key_group = l2_rows(columns([start + DK for start in group_starts], DK)).astype(jnp.bfloat16)
    value_low = columns(
        [start + 2 * DK + part * DV for start in group_starts for part in range(head_ratio)], DV
    ).astype(jnp.bfloat16)

    def per_head(tensor):
        return jnp.repeat(tensor, head_ratio, axis=0)

    query_low = per_head(query_group)
    key_low = per_head(key_group)
    query_blocks = query_low.astype(jnp.float32)
    key_blocks = key_low.astype(jnp.float32)
    value_blocks = value_low.astype(jnp.float32)
    decay_blocks = log_decay.reshape(head_count, block_count, BLOCK)
    beta_blocks = beta_gate.reshape(head_count, block_count, BLOCK)
    position = jnp.arange(BLOCK)
    lower_mask = position[:, None] >= position[None, :]
    strict_mask = position[:, None] > position[None, :]
    identity_block = jnp.eye(BLOCK, dtype=jnp.float32)
    identity_key = jnp.eye(DK, dtype=jnp.float32)
    cumulative = jnp.cumsum(decay_blocks, axis=-1)
    exponent = jnp.where(lower_mask, cumulative[..., :, None] - cumulative[..., None, :], 0.0)
    damping = jnp.where(lower_mask, jnp.exp(exponent), 0.0)
    key_gram = per_head(
        jnp.einsum("gnik,gnjk->gnij", key_group, key_group, preferred_element_type=jnp.float32)
    )
    system = identity_block + jnp.where(
        strict_mask, beta_blocks[..., :, None] * key_gram * damping, 0.0
    )
    inverse_system = unit_lower_inverse(system, identity_block)
    right_sides = jnp.concatenate(
        [
            beta_blocks[..., None] * value_blocks,
            (beta_blocks * jnp.exp(cumulative))[..., None] * key_blocks,
        ],
        -1,
    )
    solved = block_product(inverse_system, right_sides)
    fresh_values = solved[..., :DV]
    wy_weights = solved[..., DV:]
    scores = (
        per_head(
            jnp.einsum(
                "gnik,gnjk->gnij", query_group, key_group, preferred_element_type=jnp.float32
            )
        )
        * damping
    )
    query_decayed = jnp.exp(cumulative)[..., None] * query_blocks
    last_cum = cumulative[..., -1]
    key_decayed = jnp.exp(last_cum[..., None] - cumulative)[..., None] * key_blocks
    last_gain = jnp.exp(last_cum)
    block_trans = last_gain[..., None, None] * identity_key - jnp.einsum(
        "hnik,hnij->hnkj", key_decayed, wy_weights, precision=exact_matmul_mode
    )
    block_state = jnp.einsum(
        "hnik,hniv->hnkv", key_decayed, fresh_values, precision=exact_matmul_mode
    )

    lanes = lax.axis_size("tp")
    steps = block_count // lanes

    def compose(first, second):
        first_trans, first_state = first
        second_trans, second_state = second
        return (
            block_product(second_trans, first_trans),
            block_product(second_trans, first_state) + second_state,
        )

    def paired(level):
        trans, state = (
            part.reshape((head_count, part.shape[1] // 2, 2) + part.shape[2:]) for part in level
        )
        return compose((trans[:, :, 0], state[:, :, 0]), (trans[:, :, 1], state[:, :, 1]))

    level = (block_trans, block_state)
    while level[0].shape[1] > lanes:
        level = paired(level)
    lane_trans, lane_state = level
    while level[0].shape[1] > 1:
        level = paired(level)
    dev_trans, dev_state = level[0][:, 0], level[1][:, 0]
    zero_state = jnp.zeros((head_count, DK, DV), jnp.float32)

    acc_trans, acc_state = dev_trans, dev_state
    distance = 1
    while distance < lax.axis_size("ctx"):
        if 2 * distance < lax.axis_size("ctx"):
            earlier = passed_along(
                jnp.concatenate([acc_trans, acc_state], -1).astype(jnp.bfloat16), "ctx", distance
            ).astype(jnp.float32)
            composed = matmul_heads(acc_trans, earlier)
            acc_trans, acc_state = composed[..., :DK], composed[..., DK:] + acc_state
        else:
            earlier = passed_along(acc_state.astype(jnp.bfloat16), "ctx", distance)
            acc_state = matmul_heads(acc_trans, earlier.astype(jnp.float32)) + acc_state
        distance *= 2
    entering = passed_along(acc_state.astype(jnp.bfloat16), "ctx", 1).astype(jnp.float32)
    lane_entry = [entering]
    for lane in range(1, lanes):
        lane_entry.append(
            matmul_heads(lane_trans[:, lane - 1], lane_entry[-1]) + lane_state[:, lane - 1]
        )
    present_state = jnp.stack(lane_entry, 1)

    def by_step(tensor):
        return tensor.reshape((head_count, lanes, steps) + tensor.shape[2:])

    query_decayed = by_step(query_decayed)
    wy_weights = by_step(wy_weights)
    fresh_values = by_step(fresh_values)
    scores = by_step(scores)
    key_decayed = by_step(key_decayed)
    last_gain = by_step(last_gain)
    gate_values = jax.nn.silu(output_gate.astype(jnp.float32)).reshape(
        lanes, steps, BLOCK, head_count, DV
    )
    tp_index = lax.axis_index("tp")

    def summed_share(partial):
        total = lax.dynamic_index_in_dim(partial, tp_index, 0, keepdims=False).astype(jnp.float32)
        for direction in (1, -1):
            carried = None
            for stage in range(1, lanes):
                target = jnp.clip(tp_index + direction * (lanes - stage), 0, lanes - 1)
                outgoing = lax.dynamic_index_in_dim(partial, target, 0, keepdims=False)
                if carried is not None:
                    outgoing = (outgoing.astype(jnp.float32) + carried.astype(jnp.float32)).astype(
                        jnp.bfloat16
                    )
                if direction == 1:
                    route = [(i, i + 1) for i in range(stage)]
                else:
                    route = [(i, i - 1) for i in range(lanes - stage, lanes)]
                carried = lax.ppermute(outgoing, "tp", route)
            total = total + carried.astype(jnp.float32)
        return total.astype(jnp.bfloat16)

    pieces = []
    for step in range(steps):
        updated_value_rows = fresh_values[:, :, step] - block_product(
            wy_weights[:, :, step], present_state
        )
        emitted = block_product(query_decayed[:, :, step], present_state) + block_product(
            scores[:, :, step], updated_value_rows
        )
        if step + 1 < steps:
            present_state = last_gain[:, :, step][..., None, None] * present_state + jnp.einsum(
                "hnpi,hnpj->hnij",
                key_decayed[:, :, step],
                updated_value_rows,
                precision=exact_matmul_mode,
            )
        attended = emitted.transpose(1, 2, 0, 3)
        scaled = attended * lax.rsqrt(jnp.mean(attended * attended, axis=-1, keepdims=True) + 1e-06)
        normed = (
            (scaled * norm_gain * gate_values[:, step])
            .astype(jnp.bfloat16)
            .reshape(lanes * BLOCK, head_count * DV)
        )
        partial = (
            jnp.dot(normed, out_weight, preferred_element_type=jnp.float32)
            .astype(jnp.bfloat16)
            .reshape(lanes, BLOCK, -1)
        )
        if step + 1 < steps:
            present_state, partial = lax.optimization_barrier((present_state, partial))
        pieces.append(summed_share(partial))
    return jnp.concatenate(pieces, 0)


def solution(mesh):
    in_specs = (
        P("ctx", "tp"),
        P(None, "tp"),
        P("tp", "ctx"),
        P("tp", "ctx"),
        P("ctx", "tp"),
        P(),
        P("tp", None),
    )
    out_specs = P(("ctx", "tp"), None)
    return jax.shard_map(body, mesh=mesh, in_specs=in_specs, out_specs=out_specs, check_vma=False)
```

```python
import jax
import jax.numpy as jnp
from jax import lax
from jax.sharding import PartitionSpec as P

VALUE_HEADS = 32
HK = 16
DK = 128
DV = 128
KCONV = 4
BLOCK = 64


exact_matmul_mode = lax.Precision.HIGH


def passed_along(block, axis, distance):
    devices = range(lax.axis_size(axis))
    route = [(i - distance, i) for i in devices if i - distance in devices]
    return lax.ppermute(block, axis, route)


def l2_rows(tensor):
    return tensor * lax.rsqrt(jnp.sum(tensor * tensor, axis=-1, keepdims=True) + 1e-06)


def matmul_heads(former, latter):
    return jnp.einsum("hij,hjk->hik", former, latter, precision=exact_matmul_mode)


def block_product(former, latter):
    return jnp.einsum("hnij,hnjk->hnik", former, latter, precision=exact_matmul_mode)


def unit_lower_inverse(system, identity_block):
    power = identity_block - system
    inverse = identity_block + power
    for squaring in range(5):
        power = block_product(power, power)
        inverse = inverse + block_product(inverse, power)
    return inverse


def body(qkv_input, conv_weight, log_decay, beta_gate, output_gate, norm_gain, out_weight):
    tokens = qkv_input.shape[0]
    head_ratio = VALUE_HEADS // HK
    group_width = 2 * DK + head_ratio * DV
    group_count = qkv_input.shape[1] // group_width
    head_count = group_count * head_ratio
    block_count = tokens // BLOCK
    last_rows = qkv_input[tokens - (KCONV - 1) :]
    prior_rows = passed_along(last_rows, "ctx", 1)
    padded = jnp.concatenate([prior_rows, qkv_input], 0).astype(jnp.float32)
    conv_taps = conv_weight.astype(jnp.float32)
    mixed = conv_taps[0] * padded[0:tokens]
    for offset in range(1, KCONV):
        mixed = mixed + conv_taps[offset] * padded[offset : offset + tokens]
    activated = jax.nn.silu(mixed)

    def columns(starts, width):
        return jnp.stack([activated[:, start : start + width] for start in starts], 0).reshape(
            len(starts), block_count, BLOCK, width
        )

    group_starts = [group * group_width for group in range(group_count)]
    query_group = (l2_rows(columns(group_starts, DK)) * DK ** (-0.5)).astype(jnp.bfloat16)
    key_group = l2_rows(columns([start + DK for start in group_starts], DK)).astype(jnp.bfloat16)
    value_low = columns(
        [start + 2 * DK + part * DV for start in group_starts for part in range(head_ratio)], DV
    ).astype(jnp.bfloat16)

    def per_head(tensor):
        return jnp.repeat(tensor, head_ratio, axis=0)

    query_low = per_head(query_group)
    key_low = per_head(key_group)
    query_blocks = query_low.astype(jnp.float32)
    key_blocks = key_low.astype(jnp.float32)
    value_blocks = value_low.astype(jnp.float32)
    decay_blocks = log_decay.reshape(head_count, block_count, BLOCK)
    beta_blocks = beta_gate.reshape(head_count, block_count, BLOCK)
    position = jnp.arange(BLOCK)
    lower_mask = position[:, None] >= position[None, :]
    strict_mask = position[:, None] > position[None, :]
    identity_block = jnp.eye(BLOCK, dtype=jnp.float32)
    identity_key = jnp.eye(DK, dtype=jnp.float32)
    cumulative = jnp.cumsum(decay_blocks, axis=-1)
    exponent = jnp.where(lower_mask, cumulative[..., :, None] - cumulative[..., None, :], 0.0)
    damping = jnp.where(lower_mask, jnp.exp(exponent), 0.0)
    key_gram = per_head(
        jnp.einsum("gnik,gnjk->gnij", key_group, key_group, preferred_element_type=jnp.float32)
    )
    system = identity_block + jnp.where(
        strict_mask, beta_blocks[..., :, None] * key_gram * damping, 0.0
    )
    inverse_system = unit_lower_inverse(system, identity_block)
    fresh_values = block_product(inverse_system, beta_blocks[..., None] * value_blocks)
    wy_weights = block_product(
        inverse_system, (beta_blocks * jnp.exp(cumulative))[..., None] * key_blocks
    )
    scores = (
        per_head(
            jnp.einsum(
                "gnik,gnjk->gnij", query_group, key_group, preferred_element_type=jnp.float32
            )
        )
        * damping
    )
    query_decayed = jnp.exp(cumulative)[..., None] * query_blocks
    last_cum = cumulative[..., -1]
    key_decayed = jnp.exp(last_cum[..., None] - cumulative)[..., None] * key_blocks
    last_gain = jnp.exp(last_cum)
    block_trans = last_gain[..., None, None] * identity_key - jnp.einsum(
        "hnik,hnij->hnkj", key_decayed, wy_weights, precision=exact_matmul_mode
    )
    block_state = jnp.einsum(
        "hnik,hniv->hnkv", key_decayed, fresh_values, precision=exact_matmul_mode
    )

    lanes = lax.axis_size("tp")
    steps = block_count // lanes

    def compose(first, second):
        first_trans, first_state = first
        second_trans, second_state = second
        return (
            block_product(second_trans, first_trans),
            block_product(second_trans, first_state) + second_state,
        )

    def paired(level):
        trans, state = (
            part.reshape((head_count, part.shape[1] // 2, 2) + part.shape[2:]) for part in level
        )
        return compose((trans[:, :, 0], state[:, :, 0]), (trans[:, :, 1], state[:, :, 1]))

    level = (block_trans, block_state)
    while level[0].shape[1] > lanes:
        level = paired(level)
    lane_trans, lane_state = level
    while level[0].shape[1] > 1:
        level = paired(level)
    dev_trans, dev_state = level[0][:, 0], level[1][:, 0]
    zero_state = jnp.zeros((head_count, DK, DV), jnp.float32)

    acc_trans, acc_state = dev_trans, dev_state
    distance = 1
    while distance < lax.axis_size("ctx"):
        if 2 * distance < lax.axis_size("ctx"):
            earlier = passed_along(
                jnp.concatenate([acc_trans, acc_state], -1).astype(jnp.bfloat16), "ctx", distance
            ).astype(jnp.float32)
            composed = matmul_heads(acc_trans, earlier)
            acc_trans, acc_state = composed[..., :DK], composed[..., DK:] + acc_state
        else:
            earlier = passed_along(acc_state.astype(jnp.bfloat16), "ctx", distance)
            acc_state = matmul_heads(acc_trans, earlier.astype(jnp.float32)) + acc_state
        distance *= 2
    entering = passed_along(acc_state.astype(jnp.bfloat16), "ctx", 1).astype(jnp.float32)
    lane_entry = [entering]
    for lane in range(1, lanes):
        lane_entry.append(
            matmul_heads(lane_trans[:, lane - 1], lane_entry[-1]) + lane_state[:, lane - 1]
        )
    present_state = jnp.stack(lane_entry, 1)

    def by_step(tensor):
        return tensor.reshape((head_count, lanes, steps) + tensor.shape[2:])

    query_decayed = by_step(query_decayed)
    wy_weights = by_step(wy_weights)
    fresh_values = by_step(fresh_values)
    scores = by_step(scores)
    key_decayed = by_step(key_decayed)
    last_gain = by_step(last_gain)
    gate_values = jax.nn.silu(output_gate.astype(jnp.float32)).reshape(
        lanes, steps, BLOCK, head_count, DV
    )
    tp_index = lax.axis_index("tp")

    def summed_share(partial):
        total = lax.dynamic_index_in_dim(partial, tp_index, 0, keepdims=False).astype(jnp.float32)
        for direction in (1, -1):
            carried = None
            for stage in range(1, lanes):
                target = jnp.clip(tp_index + direction * (lanes - stage), 0, lanes - 1)
                outgoing = lax.dynamic_index_in_dim(partial, target, 0, keepdims=False)
                if carried is not None:
                    outgoing = (outgoing.astype(jnp.float32) + carried.astype(jnp.float32)).astype(
                        jnp.bfloat16
                    )
                if direction == 1:
                    route = [(i, i + 1) for i in range(stage)]
                else:
                    route = [(i, i - 1) for i in range(lanes - stage, lanes)]
                carried = lax.ppermute(outgoing, "tp", route)
            total = total + carried.astype(jnp.float32)
        return total.astype(jnp.bfloat16)

    pieces = []
    for step in range(steps):
        updated_value_rows = fresh_values[:, :, step] - block_product(
            wy_weights[:, :, step], present_state
        )
        emitted = block_product(query_decayed[:, :, step], present_state) + block_product(
            scores[:, :, step], updated_value_rows
        )
        if step + 1 < steps:
            present_state = last_gain[:, :, step][..., None, None] * present_state + jnp.einsum(
                "hnpi,hnpj->hnij",
                key_decayed[:, :, step],
                updated_value_rows,
                precision=exact_matmul_mode,
            )
        attended = emitted.transpose(1, 2, 0, 3)
        scaled = attended * lax.rsqrt(jnp.mean(attended * attended, axis=-1, keepdims=True) + 1e-06)
        normed = (
            (scaled * norm_gain * gate_values[:, step])
            .astype(jnp.bfloat16)
            .reshape(lanes * BLOCK, head_count * DV)
        )
        partial = (
            jnp.dot(normed, out_weight, preferred_element_type=jnp.float32)
            .astype(jnp.bfloat16)
            .reshape(lanes, BLOCK, -1)
        )
        if step + 1 < steps:
            present_state, partial = lax.optimization_barrier((present_state, partial))
        pieces.append(summed_share(partial))
    return jnp.concatenate(pieces, 0)


def solution(mesh):
    in_specs = (
        P("ctx", "tp"),
        P(None, "tp"),
        P("tp", "ctx"),
        P("tp", "ctx"),
        P("ctx", "tp"),
        P(),
        P("tp", None),
    )
    out_specs = P(("ctx", "tp"), None)
    return jax.shard_map(body, mesh=mesh, in_specs=in_specs, out_specs=out_specs, check_vma=False)
```

```python
import jax
import jax.numpy as jnp
from jax import lax
from jax.sharding import PartitionSpec as P

VALUE_HEADS = 32
HK = 16
DK = 128
DV = 128
KCONV = 4
BLOCK = 64


exact_matmul_mode = lax.Precision.HIGH


def passed_along(block, axis, distance):
    devices = range(lax.axis_size(axis))
    route = [(i - distance, i) for i in devices if i - distance in devices]
    return lax.ppermute(block, axis, route)


def l2_rows(tensor):
    return tensor * lax.rsqrt(jnp.sum(tensor * tensor, axis=-1, keepdims=True) + 1e-06)


def matmul_heads(former, latter):
    return jnp.einsum("hij,hjk->hik", former, latter, precision=exact_matmul_mode)


def block_product(former, latter):
    return jnp.einsum("hnij,hnjk->hnik", former, latter, precision=exact_matmul_mode)


def unit_lower_inverse(system, identity_block):
    power = identity_block - system
    inverse = identity_block + power
    for squaring in range(5):
        power = block_product(power, power)
        inverse = inverse + block_product(inverse, power)
    return inverse


def body(qkv_input, conv_weight, log_decay, beta_gate, output_gate, norm_gain, out_weight):
    tokens = qkv_input.shape[0]
    head_ratio = VALUE_HEADS // HK
    group_width = 2 * DK + head_ratio * DV
    group_count = qkv_input.shape[1] // group_width
    head_count = group_count * head_ratio
    block_count = tokens // BLOCK
    last_rows = qkv_input[tokens - (KCONV - 1) :]
    prior_rows = passed_along(last_rows, "ctx", 1)
    padded = jnp.concatenate([prior_rows, qkv_input], 0).astype(jnp.float32)
    conv_taps = conv_weight.astype(jnp.float32)
    mixed = conv_taps[0] * padded[0:tokens]
    for offset in range(1, KCONV):
        mixed = mixed + conv_taps[offset] * padded[offset : offset + tokens]
    activated = jax.nn.silu(mixed)

    def columns(starts, width):
        return jnp.stack([activated[:, start : start + width] for start in starts], 0).reshape(
            len(starts), block_count, BLOCK, width
        )

    group_starts = [group * group_width for group in range(group_count)]
    query_group = (l2_rows(columns(group_starts, DK)) * DK ** (-0.5)).astype(jnp.bfloat16)
    key_group = l2_rows(columns([start + DK for start in group_starts], DK)).astype(jnp.bfloat16)
    value_low = columns(
        [start + 2 * DK + part * DV for start in group_starts for part in range(head_ratio)], DV
    ).astype(jnp.bfloat16)

    def per_head(tensor):
        return jnp.repeat(tensor, head_ratio, axis=0)

    query_low = per_head(query_group)
    key_low = per_head(key_group)
    query_blocks = query_low.astype(jnp.float32)
    key_blocks = key_low.astype(jnp.float32)
    value_blocks = value_low.astype(jnp.float32)
    decay_blocks = log_decay.reshape(head_count, block_count, BLOCK)
    beta_blocks = beta_gate.reshape(head_count, block_count, BLOCK)
    position = jnp.arange(BLOCK)
    lower_mask = position[:, None] >= position[None, :]
    strict_mask = position[:, None] > position[None, :]
    identity_block = jnp.eye(BLOCK, dtype=jnp.float32)
    identity_key = jnp.eye(DK, dtype=jnp.float32)
    cumulative = jnp.cumsum(decay_blocks, axis=-1)
    exponent = jnp.where(lower_mask, cumulative[..., :, None] - cumulative[..., None, :], 0.0)
    damping = jnp.where(lower_mask, jnp.exp(exponent), 0.0)
    key_gram = per_head(
        jnp.einsum("gnik,gnjk->gnij", key_group, key_group, preferred_element_type=jnp.float32)
    )
    system = identity_block + jnp.where(
        strict_mask, beta_blocks[..., :, None] * key_gram * damping, 0.0
    )
    inverse_system = unit_lower_inverse(system, identity_block)
    fresh_values = block_product(inverse_system, beta_blocks[..., None] * value_blocks)
    wy_weights = block_product(
        inverse_system, (beta_blocks * jnp.exp(cumulative))[..., None] * key_blocks
    )
    scores = (
        per_head(
            jnp.einsum(
                "gnik,gnjk->gnij", query_group, key_group, preferred_element_type=jnp.float32
            )
        )
        * damping
    )
    query_decayed = jnp.exp(cumulative)[..., None] * query_blocks
    last_cum = cumulative[..., -1]
    key_decayed = jnp.exp(last_cum[..., None] - cumulative)[..., None] * key_blocks
    last_gain = jnp.exp(last_cum)
    block_trans = last_gain[..., None, None] * identity_key - jnp.einsum(
        "hnik,hnij->hnkj", key_decayed, wy_weights, precision=exact_matmul_mode
    )
    block_state = jnp.einsum(
        "hnik,hniv->hnkv", key_decayed, fresh_values, precision=exact_matmul_mode
    )

    lanes = lax.axis_size("tp")
    steps = block_count // lanes

    def compose(first, second):
        first_trans, first_state = first
        second_trans, second_state = second
        return (
            block_product(second_trans, first_trans),
            block_product(second_trans, first_state) + second_state,
        )

    def paired(level):
        trans, state = (
            part.reshape((head_count, part.shape[1] // 2, 2) + part.shape[2:]) for part in level
        )
        return compose((trans[:, :, 0], state[:, :, 0]), (trans[:, :, 1], state[:, :, 1]))

    level = (block_trans, block_state)
    while level[0].shape[1] > lanes:
        level = paired(level)
    lane_trans, lane_state = level
    while level[0].shape[1] > 1:
        level = paired(level)
    dev_trans, dev_state = level[0][:, 0], level[1][:, 0]
    zero_state = jnp.zeros((head_count, DK, DV), jnp.float32)

    acc_trans, acc_state = dev_trans, dev_state
    distance = 1
    while distance < lax.axis_size("ctx"):
        if 2 * distance < lax.axis_size("ctx"):
            earlier = passed_along(
                jnp.stack([acc_trans, acc_state]).astype(jnp.bfloat16), "ctx", distance
            ).astype(jnp.float32)
            composed = jnp.einsum(
                "hij,shjk->shik", acc_trans, earlier, precision=exact_matmul_mode
            )
            acc_trans, acc_state = composed[0], composed[1] + acc_state
        else:
            earlier = passed_along(acc_state.astype(jnp.bfloat16), "ctx", distance)
            acc_state = matmul_heads(acc_trans, earlier.astype(jnp.float32)) + acc_state
        distance *= 2
    entering = passed_along(acc_state.astype(jnp.bfloat16), "ctx", 1).astype(jnp.float32)
    lane_entry = [entering]
    for lane in range(1, lanes):
        lane_entry.append(
            matmul_heads(lane_trans[:, lane - 1], lane_entry[-1]) + lane_state[:, lane - 1]
        )
    present_state = jnp.stack(lane_entry, 1)

    def by_step(tensor):
        return tensor.reshape((head_count, lanes, steps) + tensor.shape[2:])

    query_decayed = by_step(query_decayed)
    wy_weights = by_step(wy_weights)
    fresh_values = by_step(fresh_values)
    scores = by_step(scores)
    key_decayed = by_step(key_decayed)
    last_gain = by_step(last_gain)
    gate_values = jax.nn.silu(output_gate.astype(jnp.float32)).reshape(
        lanes, steps, BLOCK, head_count, DV
    )
    tp_index = lax.axis_index("tp")

    def summed_share(partial):
        total = lax.dynamic_index_in_dim(partial, tp_index, 0, keepdims=False).astype(jnp.float32)
        for direction in (1, -1):
            carried = None
            for stage in range(1, lanes):
                target = jnp.clip(tp_index + direction * (lanes - stage), 0, lanes - 1)
                outgoing = lax.dynamic_index_in_dim(partial, target, 0, keepdims=False)
                if carried is not None:
                    outgoing = (outgoing.astype(jnp.float32) + carried.astype(jnp.float32)).astype(
                        jnp.bfloat16
                    )
                if direction == 1:
                    route = [(i, i + 1) for i in range(stage)]
                else:
                    route = [(i, i - 1) for i in range(lanes - stage, lanes)]
                carried = lax.ppermute(outgoing, "tp", route)
            total = total + carried.astype(jnp.float32)
        return total.astype(jnp.bfloat16)

    pieces = []
    for step in range(steps):
        updated_value_rows = fresh_values[:, :, step] - block_product(
            wy_weights[:, :, step], present_state
        )
        emitted = block_product(query_decayed[:, :, step], present_state) + block_product(
            scores[:, :, step], updated_value_rows
        )
        if step + 1 < steps:
            present_state = last_gain[:, :, step][..., None, None] * present_state + jnp.einsum(
                "hnpi,hnpj->hnij",
                key_decayed[:, :, step],
                updated_value_rows,
                precision=exact_matmul_mode,
            )
        attended = emitted.transpose(1, 2, 0, 3)
        scaled = attended * lax.rsqrt(jnp.mean(attended * attended, axis=-1, keepdims=True) + 1e-06)
        normed = (
            (scaled * norm_gain * gate_values[:, step])
            .astype(jnp.bfloat16)
            .reshape(lanes * BLOCK, head_count * DV)
        )
        partial = (
            jnp.dot(normed, out_weight, preferred_element_type=jnp.float32)
            .astype(jnp.bfloat16)
            .reshape(lanes, BLOCK, -1)
        )
        if step + 1 < steps:
            present_state, partial = lax.optimization_barrier((present_state, partial))
        pieces.append(summed_share(partial))
    return jnp.concatenate(pieces, 0)


def solution(mesh):
    in_specs = (
        P("ctx", "tp"),
        P(None, "tp"),
        P("tp", "ctx"),
        P("tp", "ctx"),
        P("ctx", "tp"),
        P(),
        P("tp", None),
    )
    out_specs = P(("ctx", "tp"), None)
    return jax.shard_map(body, mesh=mesh, in_specs=in_specs, out_specs=out_specs, check_vma=False)
```

```python
import jax
import jax.numpy as jnp
from jax import lax
from jax.sharding import PartitionSpec as P

VALUE_HEADS = 32
HK = 16
DK = 128
DV = 128
KCONV = 4
BLOCK = 64


exact_matmul_mode = lax.Precision.HIGH


def passed_along(block, axis, distance):
    devices = range(lax.axis_size(axis))
    route = [(i - distance, i) for i in devices if i - distance in devices]
    return lax.ppermute(block, axis, route)


def l2_rows(tensor):
    return tensor * lax.rsqrt(jnp.sum(tensor * tensor, axis=-1, keepdims=True) + 1e-06)


def matmul_heads(former, latter):
    return jnp.einsum("hij,hjk->hik", former, latter, precision=exact_matmul_mode)


def block_product(former, latter):
    return jnp.einsum("hnij,hnjk->hnik", former, latter, precision=exact_matmul_mode)


def unit_lower_inverse(system, identity_block):
    power = identity_block - system
    inverse = identity_block + power
    for squaring in range(5):
        power = block_product(power, power)
        inverse = inverse + block_product(inverse, power)
    return inverse


def body(qkv_input, conv_weight, log_decay, beta_gate, output_gate, norm_gain, out_weight):
    tokens = qkv_input.shape[0]
    head_ratio = VALUE_HEADS // HK
    group_width = 2 * DK + head_ratio * DV
    group_count = qkv_input.shape[1] // group_width
    head_count = group_count * head_ratio
    block_count = tokens // BLOCK
    last_rows = qkv_input[tokens - (KCONV - 1) :]
    prior_rows = passed_along(last_rows, "ctx", 1)
    padded = jnp.concatenate([prior_rows, qkv_input], 0).astype(jnp.float32)
    conv_taps = conv_weight.astype(jnp.float32)
    mixed = conv_taps[0] * padded[0:tokens]
    for offset in range(1, KCONV):
        mixed = mixed + conv_taps[offset] * padded[offset : offset + tokens]
    activated = jax.nn.silu(mixed)

    def columns(starts, width):
        return jnp.stack([activated[:, start : start + width] for start in starts], 0).reshape(
            len(starts), block_count, BLOCK, width
        )

    group_starts = [group * group_width for group in range(group_count)]
    query_group = (l2_rows(columns(group_starts, DK)) * DK ** (-0.5)).astype(jnp.bfloat16)
    key_group = l2_rows(columns([start + DK for start in group_starts], DK)).astype(jnp.bfloat16)
    value_low = columns(
        [start + 2 * DK + part * DV for start in group_starts for part in range(head_ratio)], DV
    ).astype(jnp.bfloat16)

    def per_head(tensor):
        return jnp.repeat(tensor, head_ratio, axis=0)

    query_low = per_head(query_group)
    key_low = per_head(key_group)
    query_blocks = query_low.astype(jnp.float32)
    key_blocks = key_low.astype(jnp.float32)
    value_blocks = value_low.astype(jnp.float32)
    decay_blocks = log_decay.reshape(head_count, block_count, BLOCK)
    beta_blocks = beta_gate.reshape(head_count, block_count, BLOCK)
    position = jnp.arange(BLOCK)
    lower_mask = position[:, None] >= position[None, :]
    strict_mask = position[:, None] > position[None, :]
    identity_block = jnp.eye(BLOCK, dtype=jnp.float32)
    identity_key = jnp.eye(DK, dtype=jnp.float32)
    cumulative = jnp.cumsum(decay_blocks, axis=-1)
    exponent = jnp.where(lower_mask, cumulative[..., :, None] - cumulative[..., None, :], 0.0)
    damping = jnp.where(lower_mask, jnp.exp(exponent), 0.0)
    key_gram = per_head(
        jnp.einsum("gnik,gnjk->gnij", key_group, key_group, preferred_element_type=jnp.float32)
    )
    system = identity_block + jnp.where(
        strict_mask, beta_blocks[..., :, None] * key_gram * damping, 0.0
    )
    inverse_system = unit_lower_inverse(system, identity_block)
    fresh_values = block_product(inverse_system, beta_blocks[..., None] * value_blocks)
    wy_weights = block_product(
        inverse_system, (beta_blocks * jnp.exp(cumulative))[..., None] * key_blocks
    )
    scores = (
        per_head(
            jnp.einsum(
                "gnik,gnjk->gnij", query_group, key_group, preferred_element_type=jnp.float32
            )
        )
        * damping
    )
    query_decayed = jnp.exp(cumulative)[..., None] * query_blocks
    last_cum = cumulative[..., -1]
    key_decayed = jnp.exp(last_cum[..., None] - cumulative)[..., None] * key_blocks
    last_gain = jnp.exp(last_cum)
    block_trans = last_gain[..., None, None] * identity_key - jnp.einsum(
        "hnik,hnij->hnkj", key_decayed, wy_weights, precision=exact_matmul_mode
    )
    block_state = jnp.einsum(
        "hnik,hniv->hnkv", key_decayed, fresh_values, precision=exact_matmul_mode
    )

    lanes = lax.axis_size("tp")
    steps = block_count // lanes

    def compose(first, second):
        first_trans, first_state = first
        second_trans, second_state = second
        return (
            block_product(second_trans, first_trans),
            block_product(second_trans, first_state) + second_state,
        )

    def paired(level):
        trans, state = (
            part.reshape((head_count, part.shape[1] // 2, 2) + part.shape[2:]) for part in level
        )
        return compose((trans[:, :, 0], state[:, :, 0]), (trans[:, :, 1], state[:, :, 1]))

    level = (block_trans, block_state)
    while level[0].shape[1] > lanes:
        level = paired(level)
    lane_trans, lane_state = level
    while level[0].shape[1] > 1:
        level = paired(level)
    dev_trans, dev_state = level[0][:, 0], level[1][:, 0]
    zero_state = jnp.zeros((head_count, DK, DV), jnp.float32)

    acc_trans, acc_state = dev_trans, dev_state
    distance = 1
    while distance < lax.axis_size("ctx"):
        if 2 * distance < lax.axis_size("ctx"):
            earlier = passed_along(
                jnp.stack([acc_trans, acc_state]).astype(jnp.bfloat16), "ctx", distance
            ).astype(jnp.float32)
            composed = jnp.einsum(
                "hij,shjk->shik", acc_trans, earlier, precision=exact_matmul_mode
            )
            acc_trans, acc_state = composed[0], composed[1] + acc_state
        else:
            earlier = passed_along(acc_state.astype(jnp.bfloat16), "ctx", distance)
            acc_state = matmul_heads(acc_trans, earlier.astype(jnp.float32)) + acc_state
        distance *= 2
    entering = passed_along(acc_state.astype(jnp.bfloat16), "ctx", 1).astype(jnp.float32)
    lane_entry = [entering]
    for lane in range(1, lanes):
        lane_entry.append(
            matmul_heads(lane_trans[:, lane - 1], lane_entry[-1]) + lane_state[:, lane - 1]
        )
    present_state = jnp.stack(lane_entry, 1)

    def by_step(tensor):
        return tensor.reshape((head_count, lanes, steps) + tensor.shape[2:])

    query_decayed = by_step(query_decayed)
    wy_weights = by_step(wy_weights)
    fresh_values = by_step(fresh_values)
    scores = by_step(scores)
    key_decayed = by_step(key_decayed)
    last_gain = by_step(last_gain)
    gate_values = (
        jax.nn.silu(output_gate.astype(jnp.float32))
        .reshape(lanes, steps, BLOCK, head_count, DV)
        .transpose(3, 1, 0, 2, 4)
    )
    weight_heads = out_weight.reshape(head_count, DV, -1)
    tp_index = lax.axis_index("tp")

    def summed_share(partial):
        total = lax.dynamic_index_in_dim(partial, tp_index, 0, keepdims=False).astype(jnp.float32)
        for direction in (1, -1):
            carried = None
            for stage in range(1, lanes):
                target = jnp.clip(tp_index + direction * (lanes - stage), 0, lanes - 1)
                outgoing = lax.dynamic_index_in_dim(partial, target, 0, keepdims=False)
                if carried is not None:
                    outgoing = (outgoing.astype(jnp.float32) + carried.astype(jnp.float32)).astype(
                        jnp.bfloat16
                    )
                if direction == 1:
                    route = [(i, i + 1) for i in range(stage)]
                else:
                    route = [(i, i - 1) for i in range(lanes - stage, lanes)]
                carried = lax.ppermute(outgoing, "tp", route)
            total = total + carried.astype(jnp.float32)
        return total.astype(jnp.bfloat16)

    pieces = []
    for step in range(steps):
        updated_value_rows = fresh_values[:, :, step] - block_product(
            wy_weights[:, :, step], present_state
        )
        emitted = block_product(query_decayed[:, :, step], present_state) + block_product(
            scores[:, :, step], updated_value_rows
        )
        if step + 1 < steps:
            present_state = last_gain[:, :, step][..., None, None] * present_state + jnp.einsum(
                "hnpi,hnpj->hnij",
                key_decayed[:, :, step],
                updated_value_rows,
                precision=exact_matmul_mode,
            )
        scaled = emitted * lax.rsqrt(jnp.mean(emitted * emitted, axis=-1, keepdims=True) + 1e-06)
        normed = (scaled * norm_gain * gate_values[:, step]).astype(jnp.bfloat16)
        partial = jnp.einsum(
            "hlrd,hdo->lro", normed, weight_heads, preferred_element_type=jnp.float32
        ).astype(jnp.bfloat16)
        if step + 1 < steps:
            present_state, partial = lax.optimization_barrier((present_state, partial))
        pieces.append(summed_share(partial))
    return jnp.concatenate(pieces, 0)


def solution(mesh):
    in_specs = (
        P("ctx", "tp"),
        P(None, "tp"),
        P("tp", "ctx"),
        P("tp", "ctx"),
        P("ctx", "tp"),
        P(),
        P("tp", None),
    )
    out_specs = P(("ctx", "tp"), None)
    return jax.shard_map(body, mesh=mesh, in_specs=in_specs, out_specs=out_specs, check_vma=False)
```
